256 devices in a mesh: batch: 16 (over y_hi, z), gx: 4 (over y_lo, core), gy: 4 (over x).
Axes of the slice: x: 4, y: 4 (y_hi: 2, y_lo: 2; y = y_hi * 2 + y_lo), z: 8, core: 2. Of those that a mesh axis runs over, the one named last changes fastest.
Arguments:
- features: bfloat16 [1024, 64, 4, 256], P(('batch', 'gx'), 'gy'), parts along dimension 0, may hold values from -6 to 6
- conv_weight: bfloat16 [6912, 256], replicated, may hold values from -0.078125 to 0.078125
- down_weight: bfloat16 [2048, 512], replicated, may hold values from -0.125 to 0.125
- norm_gain: float32 [512], replicated, may hold values from 0.1 to 1.9
- qkv_weight: bfloat16 [512, 1536], replicated, may hold values from -0.25 to 0.25
- out_weight: bfloat16 [512, 512], replicated, may hold values from -0.25 to 0.25
- upstream: bfloat16 [512, 32, 2, 512], P(('batch', 'gx'), 'gy'), parts along dimension 0, may hold values from -6 to 6
Outputs:
- grad_features: bfloat16 [1024, 64, 4, 256], P(('batch', 'gx'), 'gy'), parts along dimension 0
- grad_conv: bfloat16 [110592, 256], P(('batch', 'gx', 'gy')), parts along dimension 0
- grad_down: bfloat16 [32768, 512], P(('batch', 'gx', 'gy')), parts along dimension 0
- grad_gain: float32 [8192], P(('batch', 'gx', 'gy')), parts along dimension 0
- grad_qkv: bfloat16 [8192, 1536], P(('batch', 'gx', 'gy')), parts along dimension 0
- grad_out: bfloat16 [8192, 512], P(('batch', 'gx', 'gy')), parts along dimension 0
The draws below stay inside these ranges and needn't reach their ends.
There are 16 independent parts, one for each index of `batch`. The reference program is written for one: setup_inputs(seed, part) draws one part's arguments, and reference() takes and returns one part's arrays. A program takes and returns all parts, laid end to end along the dimension named above; an argument that names none is the same for every part. Nothing has to cross between parts.
All inputs are finite; a program needn't handle non-finite values.
Results may differ from the reference program's by a relative error of at most 0.02.
Values may be sent and summed in bfloat16 or wider, within the bound.
No kernel may reach another device: no remote copies, remote signals or barrier semaphores. Data moves between devices by JAX's collectives and lax.ppermute only.
A program may use at most 128 MiB of HBM per device.

```python
import jax
import jax.numpy as jnp
from jax import lax

C = 256
D = 512
H = 8
HD = 64
CX = 16
CY = 16
NZ = 4
NX = 64
NY = 64
TOKENS = 2048
N_GX = 4
N_GY = 4


def steps_of(stream_key, shape, split, smallest, top_value):
    def one(dim, parts):
        steps = jax.random.uniform(jax.random.fold_in(jax.random.fold_in(stream_key, 6), dim), (parts,), jnp.float32, smallest / len(split), top_value / len(split))
        return jnp.repeat(jnp.exp(steps), shape[dim] // parts).reshape((-1,) + (1,) * (len(shape) - dim - 1))

    level = one(*split[0])
    for cut in split[1:]:
        level = level * one(*cut)
    return level


def noise(rng, dims, scale, reach, pieces=(), kind=jnp.bfloat16):
    loudness = steps_of(rng, dims, pieces, -0.22, 0.18) if pieces else 1.0
    entries = jax.random.normal(rng, dims, jnp.float32) * scale * loudness
    return jnp.minimum(jnp.maximum(entries, -reach), reach).astype(kind)


def setup_inputs(seed: int = 0, part: int = 0) -> dict:
    arg_keys = jax.random.split(jax.random.key(seed), 8)
    part_splits = jax.random.split(jax.random.fold_in(arg_keys[7], part), 8)
    features = noise(part_splits[0], (NX, NY, NZ, C), 1.0, 6.0, ((0, 4), (1, 4)))
    conv_weight = noise(arg_keys[1], (27 * C, C), (27 * C) ** -0.5, 0.078125)
    down_weight = noise(arg_keys[2], (8 * C, D), (8 * C) ** -0.5, 0.125)
    norm_gain = jnp.clip(1.0 + 0.18 * jax.random.normal(arg_keys[3], (D,), jnp.float32), 0.1, 1.9)
    qkv_weight = noise(arg_keys[4], (D, 3 * D), D ** -0.5, 0.25)
    out_weight = noise(arg_keys[5], (D, D), D ** -0.5, 0.25)
    upstream = noise(part_splits[6], (NX // 2, NY // 2, NZ // 2, D), 1.0, 6.0, ((0, 4), (1, 4)))
    return dict(features=features, conv_weight=conv_weight, down_weight=down_weight, norm_gain=norm_gain, qkv_weight=qkv_weight, out_weight=out_weight, upstream=upstream)


precise = lax.Precision.HIGHEST

def rounded(value):
    return lax.optimization_barrier(value.astype(jnp.bfloat16)).astype(jnp.float32)

def to_tokens(volume):
    extent_x, extent_y, extent_z, channels = volume.shape
    grid = volume.reshape(extent_x // 2, 2, extent_y // 2, 2, extent_z // 2, 2, channels)
    grid = grid.transpose(0, 2, 4, 1, 3, 5, 6)
    return grid.reshape(extent_x * extent_y * extent_z // 8, 8 * channels)

def from_tokens(matrix, extent_x, extent_y, extent_z):
    channels = matrix.shape[1] // 8
    grid = matrix.reshape(extent_x // 2, extent_y // 2, extent_z // 2, 2, 2, 2, channels)
    grid = grid.transpose(0, 3, 1, 4, 2, 5, 6)
    return grid.reshape(extent_x, extent_y, extent_z, channels)

def by_tiles(rows, extent_x, extent_y, extent_z):
    width = rows.shape[1]
    grid = rows.reshape(N_GX, extent_x, N_GY, extent_y, extent_z, width)
    grid = grid.transpose(0, 2, 1, 3, 4, 5)
    return grid.reshape(N_GX * N_GY, extent_x * extent_y * extent_z, width)

def tile_sum(left, right, extent_x, extent_y, extent_z):
    left_tiles = by_tiles(left, extent_x, extent_y, extent_z)
    right_tiles = by_tiles(right, extent_x, extent_y, extent_z)
    partials = jnp.einsum('tra,trb->tab', left_tiles, right_tiles, precision=precise)
    return lax.optimization_barrier(jnp.sum(rounded(partials), axis=0))

def reference(features, conv_weight, down_weight, norm_gain, qkv_weight, out_weight, upstream):
    voxels = NX * NY * NZ
    score_scale = HD ** (-0.5)
    padded = jnp.pad(features.astype(jnp.float32), ((1, 1), (1, 1), (1, 1), (0, 0)))
    weights = conv_weight.astype(jnp.float32).reshape(27, C, C)
    offsets = [(ox, oy, oz) for ox in range(3) for oy in range(3) for oz in range(3)]
    hidden = jnp.zeros((voxels, C), jnp.float32)
    for position, (ox, oy, oz) in enumerate(offsets):
        window = padded[ox:ox + NX, oy:oy + NY, oz:oz + NZ].reshape(voxels, C)
        hidden = hidden + jnp.dot(window, weights[position], precision=precise)
    gate_sig = jax.nn.sigmoid(hidden)
    activation = rounded(hidden * gate_sig)
    tokens_in = to_tokens(activation.reshape(NX, NY, NZ, C))
    trunk_rows = jnp.dot(tokens_in, down_weight.astype(jnp.float32), precision=precise)
    mean_rows = lax.optimization_barrier(jnp.mean(trunk_rows, axis=-1, keepdims=True))
    centred = trunk_rows - mean_rows
    inverse_std = lax.rsqrt(lax.optimization_barrier(jnp.mean(centred * centred, axis=-1, keepdims=True)) + 1e-05)
    normed = centred * inverse_std
    normed_b = rounded(normed * norm_gain)
    qkv_rows = rounded(jnp.dot(normed_b, qkv_weight.astype(jnp.float32), precision=precise))
    queries = qkv_rows[:, :D].reshape(TOKENS, H, HD)
    keys_h = qkv_rows[:, D:2 * D].reshape(TOKENS, H, HD)
    values_h = qkv_rows[:, 2 * D:].reshape(TOKENS, H, HD)
    scores = jnp.einsum('ihe,jhe->hij', queries, keys_h, precision=precise) * score_scale
    exp_scores = jnp.exp(scores)
    totals = lax.optimization_barrier(jnp.sum(exp_scores, axis=-1, keepdims=True))
    attn_probs = exp_scores / totals
    probs_b = rounded(attn_probs)
    attended = rounded(jnp.einsum('hij,jhe->ihe', probs_b, values_h, precision=precise).reshape(TOKENS, D))
    cotangent = upstream.reshape(TOKENS, D).astype(jnp.float32)
    tok_x = CX // 2
    tok_y = CY // 2
    tok_z = NZ // 2
    grad_out = tile_sum(attended, cotangent, tok_x, tok_y, tok_z).astype(jnp.bfloat16)
    d_attended = rounded(jnp.dot(cotangent, out_weight.astype(jnp.float32).T, precision=precise))
    d_att_h = d_attended.reshape(TOKENS, H, HD)
    d_probs = rounded(jnp.einsum('ihe,jhe->hij', d_att_h, values_h, precision=precise))
    row_delta = lax.optimization_barrier(jnp.sum(attn_probs * d_probs, axis=-1, keepdims=True))
    d_scores = attn_probs * (d_probs - row_delta)
    d_queries = jnp.einsum('hij,jhe->ihe', d_scores, keys_h, precision=precise) * score_scale
    d_keys = jnp.einsum('hij,ihe->jhe', d_scores, queries, precision=precise) * score_scale
    d_values = jnp.einsum('hij,ihe->jhe', probs_b, d_att_h, precision=precise)
    d_qkv = rounded(jnp.concatenate([d_queries.reshape(TOKENS, D), d_keys.reshape(TOKENS, D), d_values.reshape(TOKENS, D)], axis=1))
    grad_qkv = tile_sum(normed_b, d_qkv, tok_x, tok_y, tok_z).astype(jnp.bfloat16)
    d_normed = rounded(jnp.dot(d_qkv, qkv_weight.astype(jnp.float32).T, precision=precise))
    d_hat = d_normed * norm_gain
    grad_gain = lax.optimization_barrier(jnp.sum(d_normed * normed, axis=0))
    d_trunk = cotangent + inverse_std * (d_hat - lax.optimization_barrier(jnp.mean(d_hat, axis=-1, keepdims=True)) - normed * lax.optimization_barrier(jnp.mean(d_hat * normed, axis=-1, keepdims=True)))
    grad_down = tile_sum(tokens_in, d_trunk, tok_x, tok_y, tok_z).astype(jnp.bfloat16)
    d_activation = rounded(jnp.dot(d_trunk, down_weight.astype(jnp.float32).T, precision=precise))
    d_act_grid = from_tokens(d_activation, NX, NY, NZ).reshape(voxels, C)
    d_hidden = rounded(d_act_grid * gate_sig * (1.0 + hidden * (1.0 - gate_sig)))
    d_padded = jnp.pad(d_hidden.reshape(NX, NY, NZ, C), ((1, 1), (1, 1), (1, 1), (0, 0)))
    grad_rows = []
    grad_features = jnp.zeros((voxels, C), jnp.float32)
    for position, (ox, oy, oz) in enumerate(offsets):
        window = padded[ox:ox + NX, oy:oy + NY, oz:oz + NZ].reshape(voxels, C)
        grad_rows.append(tile_sum(window, d_hidden, CX, CY, NZ))
        flipped = d_padded[2 - ox:2 - ox + NX, 2 - oy:2 - oy + NY, 2 - oz:2 - oz + NZ].reshape(voxels, C)
        grad_features = grad_features + jnp.dot(flipped, weights[position].T, precision=precise)
    grad_conv = jnp.concatenate(grad_rows, axis=0).astype(jnp.bfloat16)
    return (grad_features.reshape(NX, NY, NZ, C).astype(jnp.bfloat16), grad_conv, grad_down, grad_gain, grad_qkv, grad_out)
```

```python
import jax
import jax.numpy as jnp
from jax import lax
from jax.sharding import PartitionSpec as P

H = 8
HD = 64


precise = lax.Precision.HIGHEST


def padded_2(block, sides, width):
    for axis, dim in sides:
        count = lax.axis_size(axis)
        forward = [(i, i + 1) for i in range(count - 1)]
        backward = [(target, source) for source, target in forward]
        low = lax.ppermute(
            lax.slice_in_dim(block, block.shape[dim] - width, None, axis=dim), axis, forward
        )
        high = lax.ppermute(lax.slice_in_dim(block, 0, width, axis=dim), axis, backward)
        block = jnp.concatenate([low, block, high], axis=dim)
    return block


def to_tokens(volume):
    extent_x, extent_y, extent_z, channels = volume.shape
    grid = volume.reshape(extent_x // 2, 2, extent_y // 2, 2, extent_z // 2, 2, channels)
    grid = grid.transpose(0, 2, 4, 1, 3, 5, 6)
    return grid.reshape(extent_x * extent_y * extent_z // 8, 8 * channels)


def from_tokens(matrix, extent_x, extent_y, extent_z):
    channels = matrix.shape[1] // 8
    grid = matrix.reshape(extent_x // 2, extent_y // 2, extent_z // 2, 2, 2, 2, channels)
    grid = grid.transpose(0, 3, 1, 4, 2, 5, 6)
    return grid.reshape(extent_x, extent_y, extent_z, channels)


def gather_patches(padded, extent_x, extent_y, extent_z, flipped):
    channels = padded.shape[3]
    pieces = []
    for offset_x in range(3):
        for offset_y in range(3):
            for offset_z in range(3):
                start_x = 2 - offset_x if flipped else offset_x
                start_y = 2 - offset_y if flipped else offset_y
                start_z = 2 - offset_z if flipped else offset_z
                pieces.append(
                    padded[
                        start_x : start_x + extent_x,
                        start_y : start_y + extent_y,
                        start_z : start_z + extent_z,
                    ]
                )
    joined = jnp.concatenate(pieces, axis=3)
    return joined.reshape(extent_x * extent_y * extent_z, 27 * channels)


def local(features, conv_weight, down_weight, norm_gain, qkv_weight, out_weight, upstream):
    extent_x, extent_y, extent_z, channels = features.shape
    model_width = out_weight.shape[0]
    voxels = extent_x * extent_y * extent_z
    score_scale = HD ** (-0.5)
    padded = padded_2(features, (("gx", 0), ("gy", 1)), 1)
    padded = jnp.pad(padded, ((0, 0), (0, 0), (1, 1), (0, 0)))
    patches = gather_patches(padded, extent_x, extent_y, extent_z, False)
    hidden = jnp.dot(patches, conv_weight, preferred_element_type=jnp.float32)
    gate_sig = jax.nn.sigmoid(hidden)
    activation = (hidden * gate_sig).astype(jnp.bfloat16)
    tokens_in = to_tokens(activation.reshape(extent_x, extent_y, extent_z, channels))
    tok_count = tokens_in.shape[0]
    trunk_rows = jnp.dot(tokens_in, down_weight, preferred_element_type=jnp.float32)
    mean_rows = jnp.mean(trunk_rows, axis=-1, keepdims=True)
    centred = trunk_rows - mean_rows
    inverse_std = lax.rsqrt(jnp.mean(centred * centred, axis=-1, keepdims=True) + 1e-05)
    normed = centred * inverse_std
    normed_b = (normed * norm_gain).astype(jnp.bfloat16)
    qkv_rows = jnp.dot(normed_b, qkv_weight, preferred_element_type=jnp.float32).astype(
        jnp.bfloat16
    )
    queries = qkv_rows[:, :model_width]
    local_keys = qkv_rows[:, model_width : 2 * model_width]
    local_values = qkv_rows[:, 2 * model_width :]
    gathered = lax.all_gather(
        qkv_rows[:, model_width:], ("gx", "gy"), axis=0, tiled=True
    )
    all_keys = gathered[:, :model_width]
    all_values = gathered[:, model_width:]
    queries_h = queries.reshape(tok_count, H, HD)
    keys_h = all_keys.reshape(-1, H, HD)
    values_h = all_values.reshape(-1, H, HD)
    scores = (
        jnp.einsum("ihe,jhe->hij", queries_h, keys_h, preferred_element_type=jnp.float32)
        * score_scale
    )
    exp_scores = jnp.exp(scores)
    totals = jnp.sum(exp_scores, axis=-1)
    attn_probs = exp_scores / totals[:, :, None]
    probs_b = attn_probs.astype(jnp.bfloat16)
    attended = jnp.einsum("hij,jhe->ihe", probs_b, values_h, preferred_element_type=jnp.float32)
    attended = attended.reshape(tok_count, model_width).astype(jnp.bfloat16)
    cotangent = upstream.reshape(tok_count, model_width)
    cot_float = cotangent.astype(jnp.float32)
    out_part = jnp.einsum("td,te->de", attended, cotangent, preferred_element_type=jnp.float32)
    d_attended = jnp.dot(cotangent, out_weight.T, preferred_element_type=jnp.float32).astype(
        jnp.bfloat16
    )
    d_att_h = d_attended.reshape(tok_count, H, HD)
    d_probs = jnp.einsum("ihe,jhe->hij", d_att_h, values_h, preferred_element_type=jnp.float32)
    d_probs = d_probs.astype(jnp.bfloat16).astype(jnp.float32)
    row_delta = jnp.sum(attn_probs * d_probs, axis=-1)
    d_scores = attn_probs * (d_probs - row_delta[:, :, None])
    d_queries = (
        jnp.einsum(
            "hij,jhe->ihe", d_scores, keys_h, precision=precise, preferred_element_type=jnp.float32
        )
        * score_scale
    )
    key_term = (
        jnp.einsum(
            "hij,ihe->jhe",
            d_scores,
            queries_h,
            precision=precise,
            preferred_element_type=jnp.float32,
        )
        * score_scale
    )
    value_term = jnp.einsum("hij,ihe->jhe", probs_b, d_att_h, preferred_element_type=jnp.float32)
    key_sums = lax.psum_scatter(
        jnp.concatenate(
            [
                key_term.reshape(tok_count * lax.axis_size(("gx", "gy")), model_width),
                value_term.reshape(tok_count * lax.axis_size(("gx", "gy")), model_width),
            ],
            axis=1,
        ).astype(jnp.bfloat16),
        ("gx", "gy"),
        scatter_dimension=0,
        tiled=True,
    ).astype(jnp.float32)
    d_keys = key_sums[:, :model_width].astype(jnp.bfloat16)
    d_values = key_sums[:, model_width:].astype(jnp.bfloat16)
    d_qkv = jnp.concatenate(
        [d_queries.reshape(tok_count, model_width).astype(jnp.bfloat16), d_keys, d_values], axis=1
    )
    qkv_part = jnp.einsum("td,te->de", normed_b, d_qkv, preferred_element_type=jnp.float32)
    d_normed = (
        jnp.dot(d_qkv, qkv_weight.T, preferred_element_type=jnp.float32)
        .astype(jnp.bfloat16)
        .astype(jnp.float32)
    )
    d_hat = d_normed * norm_gain
    gain_part = jnp.sum(d_normed * normed, axis=0)
    d_trunk = cot_float + inverse_std * (
        d_hat
        - jnp.mean(d_hat, axis=-1, keepdims=True)
        - normed * jnp.mean(d_hat * normed, axis=-1, keepdims=True)
    )
    down_part = jnp.einsum(
        "tr,td->rd", tokens_in, d_trunk, precision=precise, preferred_element_type=jnp.float32
    )
    d_activation = jnp.dot(
        d_trunk, down_weight.T, precision=precise, preferred_element_type=jnp.float32
    ).astype(jnp.bfloat16)
    d_act_grid = (
        from_tokens(d_activation, extent_x, extent_y, extent_z)
        .reshape(voxels, channels)
        .astype(jnp.float32)
    )
    d_hidden = (d_act_grid * gate_sig * (1.0 + hidden * (1.0 - gate_sig))).astype(jnp.bfloat16)
    conv_part = jnp.einsum("vr,vc->rc", patches, d_hidden, preferred_element_type=jnp.float32)
    d_padded = padded_2(
        d_hidden.reshape(extent_x, extent_y, extent_z, channels), (("gx", 0), ("gy", 1)), 1
    )
    d_padded = jnp.pad(d_padded, ((0, 0), (0, 0), (1, 1), (0, 0)))
    d_patches = gather_patches(d_padded, extent_x, extent_y, extent_z, True)
    conv_flip = (
        conv_weight.reshape(27, channels, channels)
        .transpose(0, 2, 1)
        .reshape(27 * channels, channels)
    )
    grad_features = jnp.dot(d_patches, conv_flip, preferred_element_type=jnp.float32)
    grad_features = grad_features.reshape(extent_x, extent_y, extent_z, channels).astype(
        jnp.bfloat16
    )
    groups = lax.axis_size(("gx", "gy"))
    gain_rows = gain_part.reshape(groups, -1)
    gain_high = gain_rows.astype(jnp.bfloat16)
    gain_low = (gain_rows - gain_high.astype(jnp.float32)).astype(jnp.bfloat16)
    gain_pair = jnp.concatenate([gain_high, gain_low], axis=1)
    gain_pair = jnp.pad(gain_pair, ((0, 0), (0, 1024 - gain_pair.shape[1])))
    pieces = [
        conv_part.astype(jnp.bfloat16),
        down_part.astype(jnp.bfloat16),
        qkv_part.astype(jnp.bfloat16),
        out_part.astype(jnp.bfloat16),
    ]
    shapes = [piece.shape for piece in pieces]
    flat = [piece.reshape(groups, -1, 128) for piece in pieces] + [gain_pair.reshape(groups, -1, 128)]
    heights = [piece.shape[1] for piece in flat]
    joined = jnp.concatenate(flat, axis=1)
    summed = lax.psum_scatter(
        joined.reshape(-1, 128), ("gx", "gy"), scatter_dimension=0, tiled=True
    )
    summed = lax.optimization_barrier(summed)
    results = []
    offset = 0
    for height in heights:
        results.append(summed[offset : offset + height])
        offset += height
    conv_sum, down_sum, qkv_sum, out_sum = [
        piece.reshape(shape[0] // groups, shape[1]) for piece, shape in zip(results[:4], shapes)
    ]
    gain_flat = results[4].reshape(-1).astype(jnp.float32)
    half = gain_high.shape[1]
    gain_sum = gain_flat[:half] + gain_flat[half : 2 * half]
    return (
        grad_features,
        conv_sum.astype(jnp.bfloat16),
        down_sum.astype(jnp.bfloat16),
        gain_sum,
        qkv_sum.astype(jnp.bfloat16),
        out_sum.astype(jnp.bfloat16),
    )


def solution(mesh):
    placed = (
        P(("batch", "gx"), "gy", None, None),
        P(),
        P(),
        P(),
        P(),
        P(),
        P(("batch", "gx"), "gy", None, None),
    )
    return jax.shard_map(
        local,
        mesh=mesh,
        in_specs=placed,
        out_specs=(
            P(("batch", "gx"), "gy", None, None),
            P(("batch", "gx", "gy"), None),
            P(("batch", "gx", "gy"), None),
            P(("batch", "gx", "gy")),
            P(("batch", "gx", "gy"), None),
            P(("batch", "gx", "gy"), None),
        ),
        check_vma=False,
    )
```

```python
import jax
import jax.numpy as jnp
from jax import lax
from jax.sharding import PartitionSpec as P

H = 8
HD = 64


precise = lax.Precision.HIGHEST


def padded_2(block, sides, width):
    for axis, dim in sides:
        count = lax.axis_size(axis)
        forward = [(i, i + 1) for i in range(count - 1)]
        backward = [(target, source) for source, target in forward]
        low = lax.ppermute(
            lax.slice_in_dim(block, block.shape[dim] - width, None, axis=dim), axis, forward
        )
        high = lax.ppermute(lax.slice_in_dim(block, 0, width, axis=dim), axis, backward)
        block = jnp.concatenate([low, block, high], axis=dim)
    return block


def to_tokens(volume):
    extent_x, extent_y, extent_z, channels = volume.shape
    grid = volume.reshape(extent_x // 2, 2, extent_y // 2, 2, extent_z // 2, 2, channels)
    grid = grid.transpose(0, 2, 4, 1, 3, 5, 6)
    return grid.reshape(extent_x * extent_y * extent_z // 8, 8 * channels)


def from_tokens(matrix, extent_x, extent_y, extent_z):
    channels = matrix.shape[1] // 8
    grid = matrix.reshape(extent_x // 2, extent_y // 2, extent_z // 2, 2, 2, 2, channels)
    grid = grid.transpose(0, 3, 1, 4, 2, 5, 6)
    return grid.reshape(extent_x, extent_y, extent_z, channels)


def gather_patches(padded, extent_x, extent_y, extent_z, flipped):
    channels = padded.shape[3]
    pieces = []
    for offset_x in range(3):
        for offset_y in range(3):
            for offset_z in range(3):
                start_x = 2 - offset_x if flipped else offset_x
                start_y = 2 - offset_y if flipped else offset_y
                start_z = 2 - offset_z if flipped else offset_z
                pieces.append(
                    padded[
                        start_x : start_x + extent_x,
                        start_y : start_y + extent_y,
                        start_z : start_z + extent_z,
                    ]
                )
    joined = jnp.concatenate(pieces, axis=3)
    return joined.reshape(extent_x * extent_y * extent_z, 27 * channels)


def local(features, conv_weight, down_weight, norm_gain, qkv_weight, out_weight, upstream):
    extent_x, extent_y, extent_z, channels = features.shape
    model_width = out_weight.shape[0]
    voxels = extent_x * extent_y * extent_z
    score_scale = HD ** (-0.5)
    padded = padded_2(features, (("gx", 0), ("gy", 1)), 1)
    padded = jnp.pad(padded, ((0, 0), (0, 0), (1, 1), (0, 0)))
    patches = gather_patches(padded, extent_x, extent_y, extent_z, False)
    hidden = jnp.dot(patches, conv_weight, preferred_element_type=jnp.float32)
    gate_sig = jax.nn.sigmoid(hidden)
    activation = (hidden * gate_sig).astype(jnp.bfloat16)
    tokens_in = to_tokens(activation.reshape(extent_x, extent_y, extent_z, channels))
    tok_count = tokens_in.shape[0]
    trunk_rows = jnp.dot(tokens_in, down_weight, preferred_element_type=jnp.float32)
    mean_rows = jnp.mean(trunk_rows, axis=-1, keepdims=True)
    centred = trunk_rows - mean_rows
    inverse_std = lax.rsqrt(jnp.mean(centred * centred, axis=-1, keepdims=True) + 1e-05)
    normed = centred * inverse_std
    normed_b = (normed * norm_gain).astype(jnp.bfloat16)
    qkv_rows = jnp.dot(normed_b, qkv_weight, preferred_element_type=jnp.float32).astype(
        jnp.bfloat16
    )
    queries = qkv_rows[:, :model_width]
    local_keys = qkv_rows[:, model_width : 2 * model_width]
    local_values = qkv_rows[:, 2 * model_width :]
    gathered = lax.all_gather(
        qkv_rows[:, model_width:], ("gx", "gy"), axis=0, tiled=True
    )
    all_keys = gathered[:, :model_width]
    all_values = gathered[:, model_width:]
    queries_h = queries.reshape(tok_count, H, HD)
    keys_h = all_keys.reshape(-1, H, HD)
    values_h = all_values.reshape(-1, H, HD)
    scores = (
        jnp.einsum("ihe,jhe->hij", queries_h, keys_h, preferred_element_type=jnp.float32)
        * score_scale
    )
    exp_scores = jnp.exp(scores)
    totals = jnp.sum(exp_scores, axis=-1)
    attn_probs = exp_scores / totals[:, :, None]
    probs_b = attn_probs.astype(jnp.bfloat16)
    attended = jnp.einsum("hij,jhe->ihe", probs_b, values_h, preferred_element_type=jnp.float32)
    attended = attended.reshape(tok_count, model_width).astype(jnp.bfloat16)
    cotangent = upstream.reshape(tok_count, model_width)
    cot_float = cotangent.astype(jnp.float32)
    out_part = jnp.einsum("td,te->de", attended, cotangent, preferred_element_type=jnp.float32)
    d_attended = jnp.dot(cotangent, out_weight.T, preferred_element_type=jnp.float32).astype(
        jnp.bfloat16
    )
    d_att_h = d_attended.reshape(tok_count, H, HD)
    d_probs = jnp.einsum("ihe,jhe->hij", d_att_h, values_h, preferred_element_type=jnp.float32)
    d_probs = d_probs.astype(jnp.bfloat16).astype(jnp.float32)
    row_delta = jnp.sum(attn_probs * d_probs, axis=-1)
    d_scores = attn_probs * (d_probs - row_delta[:, :, None])
    d_queries = (
        jnp.einsum(
            "hij,jhe->ihe", d_scores, keys_h, precision=precise, preferred_element_type=jnp.float32
        )
        * score_scale
    )
    key_term = (
        jnp.einsum(
            "hij,ihe->jhe",
            d_scores,
            queries_h,
            precision=precise,
            preferred_element_type=jnp.float32,
        )
        * score_scale
    )
    value_term = jnp.einsum("hij,ihe->jhe", probs_b, d_att_h, preferred_element_type=jnp.float32)
    groups = lax.axis_size(("gx", "gy"))
    key_parts = jnp.concatenate(
        [
            key_term.reshape(tok_count * groups, model_width),
            value_term.reshape(tok_count * groups, model_width),
        ],
        axis=1,
    ).astype(jnp.bfloat16)
    key_parts = lax.all_to_all(key_parts, ("gx", "gy"), 0, 0, tiled=True)
    key_sums = jnp.sum(
        key_parts.reshape(groups, tok_count, 2 * model_width).astype(jnp.float32), axis=0
    )
    d_keys = key_sums[:, :model_width].astype(jnp.bfloat16)
    d_values = key_sums[:, model_width:].astype(jnp.bfloat16)
    d_qkv = jnp.concatenate(
        [d_queries.reshape(tok_count, model_width).astype(jnp.bfloat16), d_keys, d_values], axis=1
    )
    qkv_part = jnp.einsum("td,te->de", normed_b, d_qkv, preferred_element_type=jnp.float32)
    d_normed = (
        jnp.dot(d_qkv, qkv_weight.T, preferred_element_type=jnp.float32)
        .astype(jnp.bfloat16)
        .astype(jnp.float32)
    )
    d_hat = d_normed * norm_gain
    gain_part = jnp.sum(d_normed * normed, axis=0)
    d_trunk = cot_float + inverse_std * (
        d_hat
        - jnp.mean(d_hat, axis=-1, keepdims=True)
        - normed * jnp.mean(d_hat * normed, axis=-1, keepdims=True)
    )
    down_part = jnp.einsum(
        "tr,td->rd", tokens_in, d_trunk, precision=precise, preferred_element_type=jnp.float32
    )
    d_activation = jnp.dot(
        d_trunk, down_weight.T, precision=precise, preferred_element_type=jnp.float32
    ).astype(jnp.bfloat16)
    d_act_grid = (
        from_tokens(d_activation, extent_x, extent_y, extent_z)
        .reshape(voxels, channels)
        .astype(jnp.float32)
    )
    d_hidden = (d_act_grid * gate_sig * (1.0 + hidden * (1.0 - gate_sig))).astype(jnp.bfloat16)
    conv_part = jnp.einsum("vr,vc->rc", patches, d_hidden, preferred_element_type=jnp.float32)
    d_padded = padded_2(
        d_hidden.reshape(extent_x, extent_y, extent_z, channels), (("gx", 0), ("gy", 1)), 1
    )
    d_padded = jnp.pad(d_padded, ((0, 0), (0, 0), (1, 1), (0, 0)))
    d_patches = gather_patches(d_padded, extent_x, extent_y, extent_z, True)
    conv_flip = (
        conv_weight.reshape(27, channels, channels)
        .transpose(0, 2, 1)
        .reshape(27 * channels, channels)
    )
    grad_features = jnp.dot(d_patches, conv_flip, preferred_element_type=jnp.float32)
    grad_features = grad_features.reshape(extent_x, extent_y, extent_z, channels).astype(
        jnp.bfloat16
    )
    groups = lax.axis_size(("gx", "gy"))
    gain_rows = gain_part.reshape(groups, -1)
    gain_high = gain_rows.astype(jnp.bfloat16)
    gain_low = (gain_rows - gain_high.astype(jnp.float32)).astype(jnp.bfloat16)
    gain_pair = jnp.concatenate([gain_high, gain_low], axis=1)
    gain_pair = jnp.pad(gain_pair, ((0, 0), (0, 1024 - gain_pair.shape[1])))
    pieces = [
        conv_part.astype(jnp.bfloat16),
        down_part.astype(jnp.bfloat16),
        qkv_part.astype(jnp.bfloat16),
        out_part.astype(jnp.bfloat16),
    ]
    shapes = [piece.shape for piece in pieces]
    flat = [piece.reshape(groups, -1, 128) for piece in pieces] + [gain_pair.reshape(groups, -1, 128)]
    heights = [piece.shape[1] for piece in flat]
    joined = jnp.concatenate(flat, axis=1)
    summed = lax.psum_scatter(
        joined.reshape(-1, 128), ("gx", "gy"), scatter_dimension=0, tiled=True
    )
    summed = lax.optimization_barrier(summed)
    results = []
    offset = 0
    for height in heights:
        results.append(summed[offset : offset + height])
        offset += height
    conv_sum, down_sum, qkv_sum, out_sum = [
        piece.reshape(shape[0] // groups, shape[1]) for piece, shape in zip(results[:4], shapes)
    ]
    gain_flat = results[4].reshape(-1).astype(jnp.float32)
    half = gain_high.shape[1]
    gain_sum = gain_flat[:half] + gain_flat[half : 2 * half]
    return (
        grad_features,
        conv_sum.astype(jnp.bfloat16),
        down_sum.astype(jnp.bfloat16),
        gain_sum,
        qkv_sum.astype(jnp.bfloat16),
        out_sum.astype(jnp.bfloat16),
    )


def solution(mesh):
    placed = (
        P(("batch", "gx"), "gy", None, None),
        P(),
        P(),
        P(),
        P(),
        P(),
        P(("batch", "gx"), "gy", None, None),
    )
    return jax.shard_map(
        local,
        mesh=mesh,
        in_specs=placed,
        out_specs=(
            P(("batch", "gx"), "gy", None, None),
            P(("batch", "gx", "gy"), None),
            P(("batch", "gx", "gy"), None),
            P(("batch", "gx", "gy")),
            P(("batch", "gx", "gy"), None),
            P(("batch", "gx", "gy"), None),
        ),
        check_vma=False,
    )
```

```python
import jax
import jax.numpy as jnp
from jax import lax
from jax.sharding import PartitionSpec as P

H = 8
HD = 64


precise = lax.Precision.HIGHEST


def padded_2(block, sides, width):
    for axis, dim in sides:
        count = lax.axis_size(axis)
        forward = [(i, i + 1) for i in range(count - 1)]
        backward = [(target, source) for source, target in forward]
        low = lax.ppermute(
            lax.slice_in_dim(block, block.shape[dim] - width, None, axis=dim), axis, forward
        )
        high = lax.ppermute(lax.slice_in_dim(block, 0, width, axis=dim), axis, backward)
        block = jnp.concatenate([low, block, high], axis=dim)
    return block


def to_tokens(volume):
    extent_x, extent_y, extent_z, channels = volume.shape
    grid = volume.reshape(extent_x // 2, 2, extent_y // 2, 2, extent_z // 2, 2, channels)
    grid = grid.transpose(0, 2, 4, 1, 3, 5, 6)
    return grid.reshape(extent_x * extent_y * extent_z // 8, 8 * channels)


def from_tokens(matrix, extent_x, extent_y, extent_z):
    channels = matrix.shape[1] // 8
    grid = matrix.reshape(extent_x // 2, extent_y // 2, extent_z // 2, 2, 2, 2, channels)
    grid = grid.transpose(0, 3, 1, 4, 2, 5, 6)
    return grid.reshape(extent_x, extent_y, extent_z, channels)


def plane_columns(padded, extent_x, extent_y, flipped):
    channels = padded.shape[3]
    rows = extent_x * extent_y * padded.shape[2]
    pieces = []
    for offset_x in range(3):
        for offset_y in range(3):
            start_x = 2 - offset_x if flipped else offset_x
            start_y = 2 - offset_y if flipped else offset_y
            pieces.append(
                padded[start_x : start_x + extent_x, start_y : start_y + extent_y].reshape(
                    rows, channels
                )
            )
    return jnp.concatenate(pieces, axis=1)


def depth_sum(product, extent_z, channels):
    grid = product.reshape(-1, extent_z, 3, channels)
    below = jnp.pad(grid[:, :-1, 0], ((0, 0), (1, 0), (0, 0)))
    above = jnp.pad(grid[:, 1:, 2], ((0, 0), (0, 1), (0, 0)))
    return (below + grid[:, :, 1] + above).reshape(-1, channels)


def local(features, conv_weight, down_weight, norm_gain, qkv_weight, out_weight, upstream):
    extent_x, extent_y, extent_z, channels = features.shape
    model_width = out_weight.shape[0]
    voxels = extent_x * extent_y * extent_z
    score_scale = HD ** (-0.5)
    taps = conv_weight.reshape(9, 3, channels, channels)
    padded = padded_2(features, (("gx", 0), ("gy", 1)), 1)
    columns = plane_columns(padded, extent_x, extent_y, False)
    weight_fwd = taps.transpose(0, 2, 1, 3).reshape(9 * channels, 3 * channels)
    hidden = depth_sum(
        jnp.dot(columns, weight_fwd, preferred_element_type=jnp.float32), extent_z, channels
    )
    gate_sig = jax.nn.sigmoid(hidden)
    activation = (hidden * gate_sig).astype(jnp.bfloat16)
    tokens_in = to_tokens(activation.reshape(extent_x, extent_y, extent_z, channels))
    tok_count = tokens_in.shape[0]
    trunk_rows = jnp.dot(tokens_in, down_weight, preferred_element_type=jnp.float32)
    mean_rows = jnp.mean(trunk_rows, axis=-1, keepdims=True)
    centred = trunk_rows - mean_rows
    inverse_std = lax.rsqrt(jnp.mean(centred * centred, axis=-1, keepdims=True) + 1e-05)
    normed = centred * inverse_std
    normed_b = (normed * norm_gain).astype(jnp.bfloat16)
    qkv_rows = jnp.dot(normed_b, qkv_weight, preferred_element_type=jnp.float32).astype(
        jnp.bfloat16
    )
    queries = qkv_rows[:, :model_width]
    local_keys = qkv_rows[:, model_width : 2 * model_width]
    local_values = qkv_rows[:, 2 * model_width :]
    gathered = lax.all_gather(
        qkv_rows[:, model_width:], ("gx", "gy"), axis=0, tiled=True
    )
    all_keys = gathered[:, :model_width]
    all_values = gathered[:, model_width:]
    queries_h = queries.reshape(tok_count, H, HD)
    keys_h = all_keys.reshape(-1, H, HD)
    values_h = all_values.reshape(-1, H, HD)
    scores = (
        jnp.einsum("ihe,jhe->hij", queries_h, keys_h, preferred_element_type=jnp.float32)
        * score_scale
    )
    exp_scores = jnp.exp(scores)
    totals = jnp.sum(exp_scores, axis=-1)
    attn_probs = exp_scores / totals[:, :, None]
    probs_b = attn_probs.astype(jnp.bfloat16)
    attended = jnp.einsum("hij,jhe->ihe", probs_b, values_h, preferred_element_type=jnp.float32)
    attended = attended.reshape(tok_count, model_width).astype(jnp.bfloat16)
    cotangent = upstream.reshape(tok_count, model_width)
    cot_float = cotangent.astype(jnp.float32)
    out_part = jnp.einsum("td,te->de", attended, cotangent, preferred_element_type=jnp.float32)
    d_attended = jnp.dot(cotangent, out_weight.T, preferred_element_type=jnp.float32).astype(
        jnp.bfloat16
    )
    d_att_h = d_attended.reshape(tok_count, H, HD)
    d_probs = jnp.einsum("ihe,jhe->hij", d_att_h, values_h, preferred_element_type=jnp.float32)
    d_probs = d_probs.astype(jnp.bfloat16).astype(jnp.float32)
    row_delta = jnp.sum(attn_probs * d_probs, axis=-1)
    d_scores = attn_probs * (d_probs - row_delta[:, :, None])
    d_queries = (
        jnp.einsum(
            "hij,jhe->ihe", d_scores, keys_h, precision=precise, preferred_element_type=jnp.float32
        )
        * score_scale
    )
    key_term = (
        jnp.einsum(
            "hij,ihe->jhe",
            d_scores,
            queries_h,
            precision=precise,
            preferred_element_type=jnp.float32,
        )
        * score_scale
    )
    value_term = jnp.einsum("hij,ihe->jhe", probs_b, d_att_h, preferred_element_type=jnp.float32)
    groups = lax.axis_size(("gx", "gy"))
    key_parts = jnp.concatenate(
        [
            key_term.reshape(tok_count * groups, model_width),
            value_term.reshape(tok_count * groups, model_width),
        ],
        axis=1,
    ).astype(jnp.bfloat16)
    key_parts = lax.all_to_all(key_parts, ("gx", "gy"), 0, 0, tiled=True)
    key_sums = jnp.sum(
        key_parts.reshape(groups, tok_count, 2 * model_width).astype(jnp.float32), axis=0
    )
    d_keys = key_sums[:, :model_width].astype(jnp.bfloat16)
    d_values = key_sums[:, model_width:].astype(jnp.bfloat16)
    d_qkv = jnp.concatenate(
        [d_queries.reshape(tok_count, model_width).astype(jnp.bfloat16), d_keys, d_values], axis=1
    )
    qkv_part = jnp.einsum("td,te->de", normed_b, d_qkv, preferred_element_type=jnp.float32)
    d_normed = (
        jnp.dot(d_qkv, qkv_weight.T, preferred_element_type=jnp.float32)
        .astype(jnp.bfloat16)
        .astype(jnp.float32)
    )
    d_hat = d_normed * norm_gain
    gain_part = jnp.sum(d_normed * normed, axis=0)
    d_trunk = cot_float + inverse_std * (
        d_hat
        - jnp.mean(d_hat, axis=-1, keepdims=True)
        - normed * jnp.mean(d_hat * normed, axis=-1, keepdims=True)
    )
    down_part = jnp.einsum(
        "tr,td->rd", tokens_in, d_trunk, precision=precise, preferred_element_type=jnp.float32
    )
    d_activation = jnp.dot(
        d_trunk, down_weight.T, precision=precise, preferred_element_type=jnp.float32
    ).astype(jnp.bfloat16)
    d_act_grid = (
        from_tokens(d_activation, extent_x, extent_y, extent_z)
        .reshape(voxels, channels)
        .astype(jnp.float32)
    )
    d_hidden = (d_act_grid * gate_sig * (1.0 + hidden * (1.0 - gate_sig))).astype(jnp.bfloat16)
    d_depth = d_hidden.reshape(-1, extent_z, channels)
    d_shifted = jnp.concatenate(
        [
            jnp.pad(d_depth[:, 1:], ((0, 0), (0, 1), (0, 0))),
            d_depth,
            jnp.pad(d_depth[:, :-1], ((0, 0), (1, 0), (0, 0))),
        ],
        axis=2,
    ).reshape(voxels, 3 * channels)
    conv_grid = jnp.einsum("vr,vc->rc", columns, d_shifted, preferred_element_type=jnp.float32)
    conv_part = (
        conv_grid.reshape(9, channels, 3, channels)
        .transpose(0, 2, 1, 3)
        .reshape(27 * channels, channels)
    )
    d_padded = padded_2(
        d_hidden.reshape(extent_x, extent_y, extent_z, channels), (("gx", 0), ("gy", 1)), 1
    )
    d_columns = plane_columns(d_padded, extent_x, extent_y, True)
    weight_bwd = taps[:, ::-1].transpose(0, 3, 1, 2).reshape(9 * channels, 3 * channels)
    grad_features = depth_sum(
        jnp.dot(d_columns, weight_bwd, preferred_element_type=jnp.float32), extent_z, channels
    )
    grad_features = grad_features.reshape(extent_x, extent_y, extent_z, channels).astype(
        jnp.bfloat16
    )
    groups = lax.axis_size(("gx", "gy"))
    gain_rows = gain_part.reshape(groups, -1)
    gain_high = gain_rows.astype(jnp.bfloat16)
    gain_low = (gain_rows - gain_high.astype(jnp.float32)).astype(jnp.bfloat16)
    gain_pair = jnp.concatenate([gain_high, gain_low], axis=1)
    gain_pair = jnp.pad(gain_pair, ((0, 0), (0, 1024 - gain_pair.shape[1])))
    pieces = [
        conv_part.astype(jnp.bfloat16),
        down_part.astype(jnp.bfloat16),
        qkv_part.astype(jnp.bfloat16),
        out_part.astype(jnp.bfloat16),
    ]
    shapes = [piece.shape for piece in pieces]
    flat = [piece.reshape(groups, -1, 128) for piece in pieces] + [gain_pair.reshape(groups, -1, 128)]
    heights = [piece.shape[1] for piece in flat]
    joined = jnp.concatenate(flat, axis=1)
    summed = lax.psum_scatter(
        joined.reshape(-1, 128), ("gx", "gy"), scatter_dimension=0, tiled=True
    )
    summed = lax.optimization_barrier(summed)
    results = []
    offset = 0
    for height in heights:
        results.append(summed[offset : offset + height])
        offset += height
    conv_sum, down_sum, qkv_sum, out_sum = [
        piece.reshape(shape[0] // groups, shape[1]) for piece, shape in zip(results[:4], shapes)
    ]
    gain_flat = results[4].reshape(-1).astype(jnp.float32)
    half = gain_high.shape[1]
    gain_sum = gain_flat[:half] + gain_flat[half : 2 * half]
    return (
        grad_features,
        conv_sum.astype(jnp.bfloat16),
        down_sum.astype(jnp.bfloat16),
        gain_sum,
        qkv_sum.astype(jnp.bfloat16),
        out_sum.astype(jnp.bfloat16),
    )


def solution(mesh):
    placed = (
        P(("batch", "gx"), "gy", None, None),
        P(),
        P(),
        P(),
        P(),
        P(),
        P(("batch", "gx"), "gy", None, None),
    )
    return jax.shard_map(
        local,
        mesh=mesh,
        in_specs=placed,
        out_specs=(
            P(("batch", "gx"), "gy", None, None),
            P(("batch", "gx", "gy"), None),
            P(("batch", "gx", "gy"), None),
            P(("batch", "gx", "gy")),
            P(("batch", "gx", "gy"), None),
            P(("batch", "gx", "gy"), None),
        ),
        check_vma=False,
    )
```

```python
import jax
import jax.numpy as jnp
from jax import lax
from jax.sharding import PartitionSpec as P

H = 8
HD = 64


precise = lax.Precision.HIGHEST


def padded_2(block, sides, width):
    for axis, dim in sides:
        count = lax.axis_size(axis)
        forward = [(i, i + 1) for i in range(count - 1)]
        backward = [(target, source) for source, target in forward]
        low = lax.ppermute(
            lax.slice_in_dim(block, block.shape[dim] - width, None, axis=dim), axis, forward
        )
        high = lax.ppermute(lax.slice_in_dim(block, 0, width, axis=dim), axis, backward)
        block = jnp.concatenate([low, block, high], axis=dim)
    return block


def to_tokens(volume):
    extent_x, extent_y, extent_z, channels = volume.shape
    grid = volume.reshape(extent_x // 2, 2, extent_y // 2, 2, extent_z // 2, 2, channels)
    grid = grid.transpose(0, 2, 4, 1, 3, 5, 6)
    return grid.reshape(extent_x * extent_y * extent_z // 8, 8 * channels)


def from_tokens(matrix, extent_x, extent_y, extent_z):
    channels = matrix.shape[1] // 8
    grid = matrix.reshape(extent_x // 2, extent_y // 2, extent_z // 2, 2, 2, 2, channels)
    grid = grid.transpose(0, 3, 1, 4, 2, 5, 6)
    return grid.reshape(extent_x, extent_y, extent_z, channels)


def plane_columns(padded, extent_x, extent_y, flipped):
    channels = padded.shape[3]
    rows = extent_x * extent_y * padded.shape[2]
    pieces = []
    for offset_x in range(3):
        for offset_y in range(3):
            start_x = 2 - offset_x if flipped else offset_x
            start_y = 2 - offset_y if flipped else offset_y
            pieces.append(
                padded[start_x : start_x + extent_x, start_y : start_y + extent_y].reshape(
                    rows, channels
                )
            )
    return jnp.concatenate(pieces, axis=1)


def depth_sum(product, extent_z, channels, flipped):
    grid = product.reshape(-1, extent_z, 3, channels)
    first, last = (2, 0) if flipped else (0, 2)
    below = jnp.pad(grid[:, :-1, first], ((0, 0), (1, 0), (0, 0)))
    above = jnp.pad(grid[:, 1:, last], ((0, 0), (0, 1), (0, 0)))
    return (below + grid[:, :, 1] + above).reshape(-1, channels)


def local(features, conv_weight, down_weight, norm_gain, qkv_weight, out_weight, upstream):
    extent_x, extent_y, extent_z, channels = features.shape
    model_width = out_weight.shape[0]
    voxels = extent_x * extent_y * extent_z
    score_scale = HD ** (-0.5)
    taps = conv_weight.reshape(9, 3, channels, channels)
    padded = padded_2(features, (("gx", 0), ("gy", 1)), 1)
    columns = plane_columns(padded, extent_x, extent_y, False)
    weight_fwd = taps.transpose(0, 2, 1, 3).reshape(9 * channels, 3 * channels)
    hidden = depth_sum(
        jnp.dot(columns, weight_fwd, preferred_element_type=jnp.float32),
        extent_z,
        channels,
        False,
    )
    gate_sig = jax.nn.sigmoid(hidden)
    activation = (hidden * gate_sig).astype(jnp.bfloat16)
    tokens_in = to_tokens(activation.reshape(extent_x, extent_y, extent_z, channels))
    tok_count = tokens_in.shape[0]
    trunk_rows = jnp.dot(tokens_in, down_weight, preferred_element_type=jnp.float32)
    mean_rows = jnp.mean(trunk_rows, axis=-1, keepdims=True)
    centred = trunk_rows - mean_rows
    inverse_std = lax.rsqrt(jnp.mean(centred * centred, axis=-1, keepdims=True) + 1e-05)
    normed = centred * inverse_std
    normed_b = (normed * norm_gain).astype(jnp.bfloat16)
    qkv_rows = jnp.dot(normed_b, qkv_weight, preferred_element_type=jnp.float32).astype(
        jnp.bfloat16
    )
    queries = qkv_rows[:, :model_width]
    local_keys = qkv_rows[:, model_width : 2 * model_width]
    local_values = qkv_rows[:, 2 * model_width :]
    gathered = lax.all_gather(
        qkv_rows[:, model_width:], ("gx", "gy"), axis=0, tiled=True
    )
    all_keys = gathered[:, :model_width]
    all_values = gathered[:, model_width:]
    queries_h = queries.reshape(tok_count, H, HD)
    keys_h = all_keys.reshape(-1, H, HD)
    values_h = all_values.reshape(-1, H, HD)
    scores = (
        jnp.einsum("ihe,jhe->hij", queries_h, keys_h, preferred_element_type=jnp.float32)
        * score_scale
    )
    exp_scores = jnp.exp(scores)
    totals = jnp.sum(exp_scores, axis=-1)
    attn_probs = exp_scores / totals[:, :, None]
    probs_b = attn_probs.astype(jnp.bfloat16)
    attended = jnp.einsum("hij,jhe->ihe", probs_b, values_h, preferred_element_type=jnp.float32)
    attended = attended.reshape(tok_count, model_width).astype(jnp.bfloat16)
    cotangent = upstream.reshape(tok_count, model_width)
    cot_float = cotangent.astype(jnp.float32)
    out_part = jnp.einsum("td,te->de", attended, cotangent, preferred_element_type=jnp.float32)
    d_attended = jnp.dot(cotangent, out_weight.T, preferred_element_type=jnp.float32).astype(
        jnp.bfloat16
    )
    d_att_h = d_attended.reshape(tok_count, H, HD)
    d_probs = jnp.einsum("ihe,jhe->hij", d_att_h, values_h, preferred_element_type=jnp.float32)
    d_probs = d_probs.astype(jnp.bfloat16).astype(jnp.float32)
    row_delta = jnp.sum(attn_probs * d_probs, axis=-1)
    d_scores = attn_probs * (d_probs - row_delta[:, :, None])
    d_queries = (
        jnp.einsum(
            "hij,jhe->ihe", d_scores, keys_h, precision=precise, preferred_element_type=jnp.float32
        )
        * score_scale
    )
    key_term = (
        jnp.einsum(
            "hij,ihe->jhe",
            d_scores,
            queries_h,
            precision=precise,
            preferred_element_type=jnp.float32,
        )
        * score_scale
    )
    value_term = jnp.einsum("hij,ihe->jhe", probs_b, d_att_h, preferred_element_type=jnp.float32)
    groups = lax.axis_size(("gx", "gy"))
    key_parts = jnp.concatenate(
        [
            key_term.reshape(tok_count * groups, model_width),
            value_term.reshape(tok_count * groups, model_width),
        ],
        axis=1,
    ).astype(jnp.bfloat16)
    key_parts = lax.all_to_all(key_parts, ("gx", "gy"), 0, 0, tiled=True)
    key_sums = jnp.sum(
        key_parts.reshape(groups, tok_count, 2 * model_width).astype(jnp.float32), axis=0
    )
    d_keys = key_sums[:, :model_width].astype(jnp.bfloat16)
    d_values = key_sums[:, model_width:].astype(jnp.bfloat16)
    d_qkv = jnp.concatenate(
        [d_queries.reshape(tok_count, model_width).astype(jnp.bfloat16), d_keys, d_values], axis=1
    )
    qkv_part = jnp.einsum("td,te->de", normed_b, d_qkv, preferred_element_type=jnp.float32)
    d_normed = (
        jnp.dot(d_qkv, qkv_weight.T, preferred_element_type=jnp.float32)
        .astype(jnp.bfloat16)
        .astype(jnp.float32)
    )
    d_hat = d_normed * norm_gain
    gain_part = jnp.sum(d_normed * normed, axis=0)
    d_trunk = cot_float + inverse_std * (
        d_hat
        - jnp.mean(d_hat, axis=-1, keepdims=True)
        - normed * jnp.mean(d_hat * normed, axis=-1, keepdims=True)
    )
    down_part = jnp.einsum(
        "tr,td->rd", tokens_in, d_trunk, precision=precise, preferred_element_type=jnp.float32
    )
    d_activation = jnp.dot(
        d_trunk, down_weight.T, precision=precise, preferred_element_type=jnp.float32
    ).astype(jnp.bfloat16)
    d_act_grid = (
        from_tokens(d_activation, extent_x, extent_y, extent_z)
        .reshape(voxels, channels)
        .astype(jnp.float32)
    )
    d_hidden = (d_act_grid * gate_sig * (1.0 + hidden * (1.0 - gate_sig))).astype(jnp.bfloat16)
    d_depth = d_hidden.reshape(-1, extent_z, channels)
    d_shifted = jnp.concatenate(
        [
            jnp.pad(d_depth[:, 1:], ((0, 0), (0, 1), (0, 0))),
            d_depth,
            jnp.pad(d_depth[:, :-1], ((0, 0), (1, 0), (0, 0))),
        ],
        axis=2,
    ).reshape(voxels, 3 * channels)
    conv_grid = jnp.einsum("vr,vc->rc", columns, d_shifted, preferred_element_type=jnp.float32)
    conv_part = (
        conv_grid.astype(jnp.bfloat16)
        .reshape(9, channels, 3, channels)
        .transpose(0, 2, 1, 3)
        .reshape(27 * channels, channels)
    )
    d_padded = padded_2(
        d_hidden.reshape(extent_x, extent_y, extent_z, channels), (("gx", 0), ("gy", 1)), 1
    )
    d_columns = plane_columns(d_padded, extent_x, extent_y, True)
    weight_bwd = taps.transpose(0, 3, 1, 2).reshape(9 * channels, 3 * channels)
    grad_features = depth_sum(
        jnp.dot(d_columns, weight_bwd, preferred_element_type=jnp.float32),
        extent_z,
        channels,
        True,
    )
    grad_features = grad_features.reshape(extent_x, extent_y, extent_z, channels).astype(
        jnp.bfloat16
    )
    groups = lax.axis_size(("gx", "gy"))
    gain_rows = gain_part.reshape(groups, -1)
    gain_high = gain_rows.astype(jnp.bfloat16)
    gain_low = (gain_rows - gain_high.astype(jnp.float32)).astype(jnp.bfloat16)
    gain_pair = jnp.concatenate([gain_high, gain_low], axis=1)
    gain_pair = jnp.pad(gain_pair, ((0, 0), (0, 1024 - gain_pair.shape[1])))
    pieces = [
        down_part.astype(jnp.bfloat16),
        qkv_part.astype(jnp.bfloat16),
        out_part.astype(jnp.bfloat16),
    ]
    shapes = [piece.shape for piece in pieces]
    flat = [piece.reshape(groups, -1, 128) for piece in pieces] + [gain_pair.reshape(groups, -1, 128)]
    heights = [piece.shape[1] for piece in flat]
    joined = jnp.concatenate(flat, axis=1)
    summed = lax.psum_scatter(
        joined.reshape(-1, 128), ("gx", "gy"), scatter_dimension=0, tiled=True
    )
    summed = lax.optimization_barrier(summed)
    results = []
    offset = 0
    for height in heights:
        results.append(summed[offset : offset + height])
        offset += height
    down_sum, qkv_sum, out_sum = [
        piece.reshape(shape[0] // groups, shape[1]) for piece, shape in zip(results[:3], shapes)
    ]
    conv_rows = lax.all_to_all(conv_part, ("gx", "gy"), 0, 0, tiled=True)
    conv_sum = jnp.sum(
        conv_rows.reshape(groups, -1, channels).astype(jnp.float32), axis=0
    )
    gain_flat = results[3].reshape(-1).astype(jnp.float32)
    half = gain_high.shape[1]
    gain_sum = gain_flat[:half] + gain_flat[half : 2 * half]
    return (
        grad_features,
        conv_sum.astype(jnp.bfloat16),
        down_sum.astype(jnp.bfloat16),
        gain_sum,
        qkv_sum.astype(jnp.bfloat16),
        out_sum.astype(jnp.bfloat16),
    )


def solution(mesh):
    placed = (
        P(("batch", "gx"), "gy", None, None),
        P(),
        P(),
        P(),
        P(),
        P(),
        P(("batch", "gx"), "gy", None, None),
    )
    return jax.shard_map(
        local,
        mesh=mesh,
        in_specs=placed,
        out_specs=(
            P(("batch", "gx"), "gy", None, None),
            P(("batch", "gx", "gy"), None),
            P(("batch", "gx", "gy"), None),
            P(("batch", "gx", "gy")),
            P(("batch", "gx", "gy"), None),
            P(("batch", "gx", "gy"), None),
        ),
        check_vma=False,
    )
```

```python
import jax
import jax.numpy as jnp
from jax import lax
from jax.sharding import PartitionSpec as P

H = 8
HD = 64


precise = lax.Precision.HIGHEST


def padded_2(block, sides, width):
    for axis, dim in sides:
        count = lax.axis_size(axis)
        forward = [(i, i + 1) for i in range(count - 1)]
        backward = [(target, source) for source, target in forward]
        low = lax.ppermute(
            lax.slice_in_dim(block, block.shape[dim] - width, None, axis=dim), axis, forward
        )
        high = lax.ppermute(lax.slice_in_dim(block, 0, width, axis=dim), axis, backward)
        block = jnp.concatenate([low, block, high], axis=dim)
    return block


def to_tokens(volume):
    extent_x, extent_y, extent_z, channels = volume.shape
    grid = volume.reshape(extent_x // 2, 2, extent_y // 2, 2, extent_z // 2, 2, channels)
    grid = grid.transpose(0, 2, 4, 1, 3, 5, 6)
    return grid.reshape(extent_x * extent_y * extent_z // 8, 8 * channels)


def from_tokens(matrix, extent_x, extent_y, extent_z):
    channels = matrix.shape[1] // 8
    grid = matrix.reshape(extent_x // 2, extent_y // 2, extent_z // 2, 2, 2, 2, channels)
    grid = grid.transpose(0, 3, 1, 4, 2, 5, 6)
    return grid.reshape(extent_x, extent_y, extent_z, channels)


def plane_columns(padded, extent_x, extent_y, flipped):
    channels = padded.shape[3]
    rows = extent_x * extent_y * padded.shape[2]
    pieces = []
    for offset_x in range(3):
        for offset_y in range(3):
            start_x = 2 - offset_x if flipped else offset_x
            start_y = 2 - offset_y if flipped else offset_y
            pieces.append(
                padded[start_x : start_x + extent_x, start_y : start_y + extent_y].reshape(
                    rows, channels
                )
            )
    return jnp.concatenate(pieces, axis=1)


def depth_sum(product, extent_z, channels, flipped):
    grid = product.reshape(-1, extent_z, 3, channels)
    first, last = (2, 0) if flipped else (0, 2)
    below = jnp.pad(grid[:, :-1, first], ((0, 0), (1, 0), (0, 0)))
    above = jnp.pad(grid[:, 1:, last], ((0, 0), (0, 1), (0, 0)))
    return (below + grid[:, :, 1] + above).reshape(-1, channels)


def local(features, conv_weight, down_weight, norm_gain, qkv_weight, out_weight, upstream):
    extent_x, extent_y, extent_z, channels = features.shape
    model_width = out_weight.shape[0]
    voxels = extent_x * extent_y * extent_z
    score_scale = HD ** (-0.5)
    taps = conv_weight.reshape(9, 3, channels, channels)
    padded = padded_2(features, (("gx", 0), ("gy", 1)), 1)
    columns = plane_columns(padded, extent_x, extent_y, False)
    weight_fwd = taps.transpose(0, 2, 1, 3).reshape(9 * channels, 3 * channels)
    hidden = depth_sum(
        jnp.dot(columns, weight_fwd, preferred_element_type=jnp.float32),
        extent_z,
        channels,
        False,
    )
    gate_sig = jax.nn.sigmoid(hidden)
    activation = (hidden * gate_sig).astype(jnp.bfloat16)
    tokens_in = to_tokens(activation.reshape(extent_x, extent_y, extent_z, channels))
    tok_count = tokens_in.shape[0]
    trunk_rows = jnp.dot(tokens_in, down_weight, preferred_element_type=jnp.float32)
    mean_rows = jnp.mean(trunk_rows, axis=-1, keepdims=True)
    centred = trunk_rows - mean_rows
    inverse_std = lax.rsqrt(jnp.mean(centred * centred, axis=-1, keepdims=True) + 1e-05)
    normed = centred * inverse_std
    normed_b = (normed * norm_gain).astype(jnp.bfloat16)
    qkv_rows = jnp.dot(normed_b, qkv_weight, preferred_element_type=jnp.float32).astype(
        jnp.bfloat16
    )
    queries = qkv_rows[:, :model_width]
    local_keys = qkv_rows[:, model_width : 2 * model_width]
    local_values = qkv_rows[:, 2 * model_width :]
    gathered = lax.all_gather(
        qkv_rows[:, model_width:], ("gx", "gy"), axis=0, tiled=True
    )
    all_keys = gathered[:, :model_width]
    all_values = gathered[:, model_width:]
    queries_h = queries.reshape(tok_count, H, HD)
    keys_h = all_keys.reshape(-1, H, HD)
    values_h = all_values.reshape(-1, H, HD)
    scores = (
        jnp.einsum("ihe,jhe->hij", queries_h, keys_h, preferred_element_type=jnp.float32)
        * score_scale
    )
    exp_scores = jnp.exp(scores)
    totals = jnp.sum(exp_scores, axis=-1)
    attn_probs = exp_scores / totals[:, :, None]
    probs_b = attn_probs.astype(jnp.bfloat16)
    attended = jnp.einsum("hij,jhe->ihe", probs_b, values_h, preferred_element_type=jnp.float32)
    attended = attended.reshape(tok_count, model_width).astype(jnp.bfloat16)
    cotangent = upstream.reshape(tok_count, model_width)
    cot_float = cotangent.astype(jnp.float32)
    out_part = jnp.einsum("td,te->de", attended, cotangent, preferred_element_type=jnp.float32)
    d_attended = jnp.dot(cotangent, out_weight.T, preferred_element_type=jnp.float32).astype(
        jnp.bfloat16
    )
    d_att_h = d_attended.reshape(tok_count, H, HD)
    d_probs = jnp.einsum("ihe,jhe->hij", d_att_h, values_h, preferred_element_type=jnp.float32)
    d_probs = d_probs.astype(jnp.bfloat16).astype(jnp.float32)
    row_delta = jnp.sum(attn_probs * d_probs, axis=-1)
    d_scores = attn_probs * (d_probs - row_delta[:, :, None])
    d_queries = (
        jnp.einsum(
            "hij,jhe->ihe", d_scores, keys_h, precision=precise, preferred_element_type=jnp.float32
        )
        * score_scale
    )
    key_term = (
        jnp.einsum(
            "hij,ihe->jhe",
            d_scores,
            queries_h,
            precision=precise,
            preferred_element_type=jnp.float32,
        )
        * score_scale
    )
    value_term = jnp.einsum("hij,ihe->jhe", probs_b, d_att_h, preferred_element_type=jnp.float32)
    groups = lax.axis_size(("gx", "gy"))
    key_parts = jnp.concatenate(
        [
            key_term.reshape(tok_count * groups, model_width),
            value_term.reshape(tok_count * groups, model_width),
        ],
        axis=1,
    ).astype(jnp.bfloat16)
    key_parts = lax.all_to_all(key_parts, ("gx", "gy"), 0, 0, tiled=True)
    key_sums = jnp.sum(
        key_parts.reshape(groups, tok_count, 2 * model_width).astype(jnp.float32), axis=0
    )
    d_keys = key_sums[:, :model_width].astype(jnp.bfloat16)
    d_values = key_sums[:, model_width:].astype(jnp.bfloat16)
    d_qkv = jnp.concatenate(
        [d_queries.reshape(tok_count, model_width).astype(jnp.bfloat16), d_keys, d_values], axis=1
    )
    qkv_part = jnp.einsum("td,te->de", normed_b, d_qkv, preferred_element_type=jnp.float32)
    d_normed = (
        jnp.dot(d_qkv, qkv_weight.T, preferred_element_type=jnp.float32)
        .astype(jnp.bfloat16)
        .astype(jnp.float32)
    )
    d_hat = d_normed * norm_gain
    gain_part = jnp.sum(d_normed * normed, axis=0)
    d_trunk = cot_float + inverse_std * (
        d_hat
        - jnp.mean(d_hat, axis=-1, keepdims=True)
        - normed * jnp.mean(d_hat * normed, axis=-1, keepdims=True)
    )
    down_part = jnp.einsum(
        "tr,td->rd", tokens_in, d_trunk, precision=precise, preferred_element_type=jnp.float32
    )
    d_activation = jnp.dot(
        d_trunk, down_weight.T, precision=precise, preferred_element_type=jnp.float32
    ).astype(jnp.bfloat16)
    d_act_grid = (
        from_tokens(d_activation, extent_x, extent_y, extent_z)
        .reshape(voxels, channels)
        .astype(jnp.float32)
    )
    d_hidden = (d_act_grid * gate_sig * (1.0 + hidden * (1.0 - gate_sig))).astype(jnp.bfloat16)
    d_depth = d_hidden.reshape(-1, extent_z, channels)
    d_shifts = [
        jnp.pad(d_depth[:, 1:], ((0, 0), (0, 1), (0, 0))),
        d_depth,
        jnp.pad(d_depth[:, :-1], ((0, 0), (1, 0), (0, 0))),
    ]
    conv_blocks = [
        jnp.einsum(
            "vr,vc->rc",
            columns,
            shifted.reshape(voxels, channels),
            preferred_element_type=jnp.float32,
        )
        .astype(jnp.bfloat16)
        .reshape(9, channels, channels)
        for shifted in d_shifts
    ]
    conv_part = jnp.stack(conv_blocks, axis=1).reshape(27 * channels, channels)
    conv_part, d_hidden = lax.optimization_barrier((conv_part, d_hidden))
    d_padded = padded_2(
        d_hidden.reshape(extent_x, extent_y, extent_z, channels), (("gx", 0), ("gy", 1)), 1
    )
    d_columns = plane_columns(d_padded, extent_x, extent_y, True)
    weight_bwd = taps.transpose(0, 3, 1, 2).reshape(9 * channels, 3 * channels)
    grad_features = depth_sum(
        jnp.dot(d_columns, weight_bwd, preferred_element_type=jnp.float32),
        extent_z,
        channels,
        True,
    )
    grad_features = grad_features.reshape(extent_x, extent_y, extent_z, channels).astype(
        jnp.bfloat16
    )
    groups = lax.axis_size(("gx", "gy"))
    gain_rows = gain_part.reshape(groups, -1)
    gain_high = gain_rows.astype(jnp.bfloat16)
    gain_low = (gain_rows - gain_high.astype(jnp.float32)).astype(jnp.bfloat16)
    gain_pair = jnp.concatenate([gain_high, gain_low], axis=1)
    gain_pair = jnp.pad(gain_pair, ((0, 0), (0, 1024 - gain_pair.shape[1])))
    pieces = [
        down_part.astype(jnp.bfloat16),
        qkv_part.astype(jnp.bfloat16),
        out_part.astype(jnp.bfloat16),
    ]
    shapes = [piece.shape for piece in pieces]
    flat = [piece.reshape(groups, -1, 128) for piece in pieces] + [gain_pair.reshape(groups, -1, 128)]
    heights = [piece.shape[1] for piece in flat]
    joined = jnp.concatenate(flat, axis=1)
    summed = lax.psum_scatter(
        joined.reshape(-1, 128), ("gx", "gy"), scatter_dimension=0, tiled=True
    )
    summed = lax.optimization_barrier(summed)
    results = []
    offset = 0
    for height in heights:
        results.append(summed[offset : offset + height])
        offset += height
    down_sum, qkv_sum, out_sum = [
        piece.reshape(shape[0] // groups, shape[1]) for piece, shape in zip(results[:3], shapes)
    ]
    conv_rows = lax.all_to_all(conv_part, ("gx", "gy"), 0, 0, tiled=True)
    conv_sum = jnp.sum(
        conv_rows.reshape(groups, -1, channels).astype(jnp.float32), axis=0
    )
    gain_flat = results[3].reshape(-1).astype(jnp.float32)
    half = gain_high.shape[1]
    gain_sum = gain_flat[:half] + gain_flat[half : 2 * half]
    return (
        grad_features,
        conv_sum.astype(jnp.bfloat16),
        down_sum.astype(jnp.bfloat16),
        gain_sum,
        qkv_sum.astype(jnp.bfloat16),
        out_sum.astype(jnp.bfloat16),
    )


def solution(mesh):
    placed = (
        P(("batch", "gx"), "gy", None, None),
        P(),
        P(),
        P(),
        P(),
        P(),
        P(("batch", "gx"), "gy", None, None),
    )
    return jax.shard_map(
        local,
        mesh=mesh,
        in_specs=placed,
        out_specs=(
            P(("batch", "gx"), "gy", None, None),
            P(("batch", "gx", "gy"), None),
            P(("batch", "gx", "gy"), None),
            P(("batch", "gx", "gy")),
            P(("batch", "gx", "gy"), None),
            P(("batch", "gx", "gy"), None),
        ),
        check_vma=False,
    )
```

```python
import jax
import jax.numpy as jnp
from jax import lax
from jax.sharding import PartitionSpec as P

H = 8
HD = 64


precise = lax.Precision.HIGHEST


def padded_2(block, sides, width):
    for axis, dim in sides:
        count = lax.axis_size(axis)
        forward = [(i, i + 1) for i in range(count - 1)]
        backward = [(target, source) for source, target in forward]
        low = lax.ppermute(
            lax.slice_in_dim(block, block.shape[dim] - width, None, axis=dim), axis, forward
        )
        high = lax.ppermute(lax.slice_in_dim(block, 0, width, axis=dim), axis, backward)
        block = jnp.concatenate([low, block, high], axis=dim)
    return block


def to_tokens(volume):
    extent_x, extent_y, extent_z, channels = volume.shape
    grid = volume.reshape(extent_x // 2, 2, extent_y // 2, 2, extent_z // 2, 2, channels)
    grid = grid.transpose(0, 2, 4, 1, 3, 5, 6)
    return grid.reshape(extent_x * extent_y * extent_z // 8, 8 * channels)


def from_tokens(matrix, extent_x, extent_y, extent_z):
    channels = matrix.shape[1] // 8
    grid = matrix.reshape(extent_x // 2, extent_y // 2, extent_z // 2, 2, 2, 2, channels)
    grid = grid.transpose(0, 3, 1, 4, 2, 5, 6)
    return grid.reshape(extent_x, extent_y, extent_z, channels)


def plane_columns(padded, extent_x, extent_y, flipped):
    channels = padded.shape[3]
    rows = extent_x * extent_y * padded.shape[2]
    pieces = []
    for offset_x in range(3):
        for offset_y in range(3):
            start_x = 2 - offset_x if flipped else offset_x
            start_y = 2 - offset_y if flipped else offset_y
            pieces.append(
                padded[start_x : start_x + extent_x, start_y : start_y + extent_y].reshape(
                    rows, channels
                )
            )
    return jnp.concatenate(pieces, axis=1)


def depth_sum(product, extent_z, channels, flipped):
    grid = product.reshape(-1, extent_z, 3, channels)
    first, last = (2, 0) if flipped else (0, 2)
    below = jnp.pad(grid[:, :-1, first], ((0, 0), (1, 0), (0, 0)))
    above = jnp.pad(grid[:, 1:, last], ((0, 0), (0, 1), (0, 0)))
    return (below + grid[:, :, 1] + above).reshape(-1, channels)


def local(features, conv_weight, down_weight, norm_gain, qkv_weight, out_weight, upstream):
    extent_x, extent_y, extent_z, channels = features.shape
    model_width = out_weight.shape[0]
    voxels = extent_x * extent_y * extent_z
    score_scale = HD ** (-0.5)
    taps = conv_weight.reshape(9, 3, channels, channels)
    padded = padded_2(features, (("gx", 0), ("gy", 1)), 1)
    columns = plane_columns(padded, extent_x, extent_y, False)
    weight_fwd = taps.transpose(0, 2, 1, 3).reshape(9 * channels, 3 * channels)
    hidden = depth_sum(
        jnp.dot(columns, weight_fwd, preferred_element_type=jnp.float32),
        extent_z,
        channels,
        False,
    )
    gate_sig = jax.nn.sigmoid(hidden)
    activation = (hidden * gate_sig).astype(jnp.bfloat16)
    tokens_in = to_tokens(activation.reshape(extent_x, extent_y, extent_z, channels))
    tok_count = tokens_in.shape[0]
    trunk_rows = jnp.dot(tokens_in, down_weight, preferred_element_type=jnp.float32)
    mean_rows = jnp.mean(trunk_rows, axis=-1, keepdims=True)
    centred = trunk_rows - mean_rows
    inverse_std = lax.rsqrt(jnp.mean(centred * centred, axis=-1, keepdims=True) + 1e-05)
    normed = centred * inverse_std
    normed_b = (normed * norm_gain).astype(jnp.bfloat16)
    qkv_rows = jnp.dot(normed_b, qkv_weight, preferred_element_type=jnp.float32).astype(
        jnp.bfloat16
    )
    queries = qkv_rows[:, :model_width]
    local_keys = qkv_rows[:, model_width : 2 * model_width]
    local_values = qkv_rows[:, 2 * model_width :]
    gathered = lax.all_gather(
        qkv_rows[:, model_width:], ("gx", "gy"), axis=0, tiled=True
    )
    all_keys = gathered[:, :model_width]
    all_values = gathered[:, model_width:]
    queries_h = queries.reshape(tok_count, H, HD)
    keys_h = all_keys.reshape(-1, H, HD)
    values_h = all_values.reshape(-1, H, HD)
    scores = (
        jnp.einsum("ihe,jhe->hij", queries_h, keys_h, preferred_element_type=jnp.float32)
        * score_scale
    )
    exp_scores = jnp.exp(scores)
    totals = jnp.sum(exp_scores, axis=-1)
    attn_probs = exp_scores / totals[:, :, None]
    probs_b = attn_probs.astype(jnp.bfloat16)
    attended = jnp.einsum("hij,jhe->ihe", probs_b, values_h, preferred_element_type=jnp.float32)
    attended = attended.reshape(tok_count, model_width).astype(jnp.bfloat16)
    cotangent = upstream.reshape(tok_count, model_width)
    cot_float = cotangent.astype(jnp.float32)
    out_part = jnp.einsum("td,te->de", attended, cotangent, preferred_element_type=jnp.float32)
    d_attended = jnp.dot(cotangent, out_weight.T, preferred_element_type=jnp.float32).astype(
        jnp.bfloat16
    )
    d_att_h = d_attended.reshape(tok_count, H, HD)
    d_probs = jnp.einsum("ihe,jhe->hij", d_att_h, values_h, preferred_element_type=jnp.float32)
    d_probs = d_probs.astype(jnp.bfloat16).astype(jnp.float32)
    row_delta = jnp.sum(attn_probs * d_probs, axis=-1)
    d_scores = attn_probs * (d_probs - row_delta[:, :, None])
    d_queries = (
        jnp.einsum(
            "hij,jhe->ihe", d_scores, keys_h, precision=precise, preferred_element_type=jnp.float32
        )
        * score_scale
    )
    key_term = (
        jnp.einsum(
            "hij,ihe->jhe",
            d_scores,
            queries_h,
            precision=precise,
            preferred_element_type=jnp.float32,
        )
        * score_scale
    )
    value_term = jnp.einsum("hij,ihe->jhe", probs_b, d_att_h, preferred_element_type=jnp.float32)
    groups = lax.axis_size(("gx", "gy"))
    key_parts = jnp.concatenate(
        [
            key_term.reshape(tok_count * groups, model_width),
            value_term.reshape(tok_count * groups, model_width),
        ],
        axis=1,
    ).astype(jnp.bfloat16)
    key_parts = lax.all_to_all(key_parts, ("gx", "gy"), 0, 0, tiled=True)
    key_sums = jnp.sum(
        key_parts.reshape(groups, tok_count, 2 * model_width).astype(jnp.float32), axis=0
    )
    d_keys = key_sums[:, :model_width].astype(jnp.bfloat16)
    d_values = key_sums[:, model_width:].astype(jnp.bfloat16)
    d_qkv = jnp.concatenate(
        [d_queries.reshape(tok_count, model_width).astype(jnp.bfloat16), d_keys, d_values], axis=1
    )
    qkv_part = jnp.einsum("td,te->de", normed_b, d_qkv, preferred_element_type=jnp.float32)
    d_normed = (
        jnp.dot(d_qkv, qkv_weight.T, preferred_element_type=jnp.float32)
        .astype(jnp.bfloat16)
        .astype(jnp.float32)
    )
    d_hat = d_normed * norm_gain
    gain_part = jnp.sum(d_normed * normed, axis=0)
    d_trunk = cot_float + inverse_std * (
        d_hat
        - jnp.mean(d_hat, axis=-1, keepdims=True)
        - normed * jnp.mean(d_hat * normed, axis=-1, keepdims=True)
    )
    down_part = jnp.einsum(
        "tr,td->rd", tokens_in, d_trunk, precision=precise, preferred_element_type=jnp.float32
    )
    d_activation = jnp.dot(
        d_trunk, down_weight.T, precision=precise, preferred_element_type=jnp.float32
    ).astype(jnp.bfloat16)
    d_act_grid = (
        from_tokens(d_activation, extent_x, extent_y, extent_z)
        .reshape(voxels, channels)
        .astype(jnp.float32)
    )
    d_hidden = (d_act_grid * gate_sig * (1.0 + hidden * (1.0 - gate_sig))).astype(jnp.bfloat16)
    d_depth = d_hidden.reshape(-1, extent_z, channels)
    d_shifts = [
        jnp.pad(d_depth[:, 1:], ((0, 0), (0, 1), (0, 0))),
        d_depth,
        jnp.pad(d_depth[:, :-1], ((0, 0), (1, 0), (0, 0))),
    ]
    conv_blocks = [
        jnp.einsum(
            "vr,vc->rc",
            columns,
            shifted.reshape(voxels, channels),
            preferred_element_type=jnp.float32,
        )
        .astype(jnp.bfloat16)
        .reshape(9, channels, channels)
        for shifted in d_shifts
    ]
    conv_part = jnp.stack(conv_blocks, axis=1).reshape(27 * channels, channels)
    d_padded = padded_2(
        d_hidden.reshape(extent_x, extent_y, extent_z, channels), (("gx", 0), ("gy", 1)), 1
    )
    d_columns = plane_columns(d_padded, extent_x, extent_y, True)
    weight_bwd = taps.transpose(0, 3, 1, 2).reshape(9 * channels, 3 * channels)
    grad_features = depth_sum(
        jnp.dot(d_columns, weight_bwd, preferred_element_type=jnp.float32),
        extent_z,
        channels,
        True,
    )
    grad_features = grad_features.reshape(extent_x, extent_y, extent_z, channels).astype(
        jnp.bfloat16
    )
    groups = lax.axis_size(("gx", "gy"))
    gain_rows = gain_part.reshape(groups, -1)
    gain_high = gain_rows.astype(jnp.bfloat16)
    gain_low = (gain_rows - gain_high.astype(jnp.float32)).astype(jnp.bfloat16)
    gain_pair = jnp.concatenate([gain_high, gain_low], axis=1)
    gain_pair = jnp.pad(gain_pair, ((0, 0), (0, 1024 - gain_pair.shape[1])))
    pieces = [
        down_part.astype(jnp.bfloat16),
        qkv_part.astype(jnp.bfloat16),
        out_part.astype(jnp.bfloat16),
    ]
    shapes = [piece.shape for piece in pieces]
    flat = [piece.reshape(groups, -1, 128) for piece in pieces] + [gain_pair.reshape(groups, -1, 128)]
    heights = [piece.shape[1] for piece in flat]
    joined = jnp.concatenate(flat, axis=1)
    summed = lax.psum_scatter(
        joined.reshape(-1, 128), ("gx", "gy"), scatter_dimension=0, tiled=True
    )
    summed = lax.optimization_barrier(summed)
    results = []
    offset = 0
    for height in heights:
        results.append(summed[offset : offset + height])
        offset += height
    down_sum, qkv_sum, out_sum = [
        piece.reshape(shape[0] // groups, shape[1]) for piece, shape in zip(results[:3], shapes)
    ]
    conv_rows = lax.all_to_all(conv_part, ("gx", "gy"), 0, 0, tiled=True)
    conv_sum = jnp.sum(
        conv_rows.reshape(groups, -1, channels).astype(jnp.float32), axis=0
    )
    gain_flat = results[3].reshape(-1).astype(jnp.float32)
    half = gain_high.shape[1]
    gain_sum = gain_flat[:half] + gain_flat[half : 2 * half]
    return (
        grad_features,
        conv_sum.astype(jnp.bfloat16),
        down_sum.astype(jnp.bfloat16),
        gain_sum,
        qkv_sum.astype(jnp.bfloat16),
        out_sum.astype(jnp.bfloat16),
    )


def solution(mesh):
    placed = (
        P(("batch", "gx"), "gy", None, None),
        P(),
        P(),
        P(),
        P(),
        P(),
        P(("batch", "gx"), "gy", None, None),
    )
    return jax.shard_map(
        local,
        mesh=mesh,
        in_specs=placed,
        out_specs=(
            P(("batch", "gx"), "gy", None, None),
            P(("batch", "gx", "gy"), None),
            P(("batch", "gx", "gy"), None),
            P(("batch", "gx", "gy")),
            P(("batch", "gx", "gy"), None),
            P(("batch", "gx", "gy"), None),
        ),
        check_vma=False,
    )
```

```python
import jax
import jax.numpy as jnp
from jax import lax
from jax.sharding import PartitionSpec as P

H = 8
HD = 64


precise = lax.Precision.HIGHEST


def padded_2(block, sides, width):
    for axis, dim in sides:
        count = lax.axis_size(axis)
        forward = [(i, i + 1) for i in range(count - 1)]
        backward = [(target, source) for source, target in forward]
        low = lax.ppermute(
            lax.slice_in_dim(block, block.shape[dim] - width, None, axis=dim), axis, forward
        )
        high = lax.ppermute(lax.slice_in_dim(block, 0, width, axis=dim), axis, backward)
        block = jnp.concatenate([low, block, high], axis=dim)
    return block


def to_tokens(volume):
    extent_x, extent_y, extent_z, channels = volume.shape
    grid = volume.reshape(extent_x // 2, 2, extent_y // 2, 2, extent_z // 2, 2, channels)
    grid = grid.transpose(0, 2, 4, 1, 3, 5, 6)
    return grid.reshape(extent_x * extent_y * extent_z // 8, 8 * channels)


def from_tokens(matrix, extent_x, extent_y, extent_z):
    channels = matrix.shape[1] // 8
    grid = matrix.reshape(extent_x // 2, extent_y // 2, extent_z // 2, 2, 2, 2, channels)
    grid = grid.transpose(0, 3, 1, 4, 2, 5, 6)
    return grid.reshape(extent_x, extent_y, extent_z, channels)


def plane_columns(padded, extent_x, extent_y, flipped):
    channels = padded.shape[3]
    rows = extent_x * extent_y * padded.shape[2]
    pieces = []
    for offset_x in range(3):
        for offset_y in range(3):
            start_x = 2 - offset_x if flipped else offset_x
            start_y = 2 - offset_y if flipped else offset_y
            pieces.append(
                padded[start_x : start_x + extent_x, start_y : start_y + extent_y].reshape(
                    rows, channels
                )
            )
    return jnp.concatenate(pieces, axis=1)


def depth_sum(product, extent_z, channels, flipped):
    grid = product.reshape(-1, extent_z, 3, channels)
    first, last = (2, 0) if flipped else (0, 2)
    below = jnp.pad(grid[:, :-1, first], ((0, 0), (1, 0), (0, 0)))
    above = jnp.pad(grid[:, 1:, last], ((0, 0), (0, 1), (0, 0)))
    return (below + grid[:, :, 1] + above).reshape(-1, channels)


def local(features, conv_weight, down_weight, norm_gain, qkv_weight, out_weight, upstream):
    extent_x, extent_y, extent_z, channels = features.shape
    model_width = out_weight.shape[0]
    voxels = extent_x * extent_y * extent_z
    score_scale = HD ** (-0.5)
    taps = conv_weight.reshape(9, 3, channels, channels)
    padded = padded_2(features, (("gx", 0), ("gy", 1)), 1)
    columns = plane_columns(padded, extent_x, extent_y, False)
    weight_fwd = taps.transpose(0, 2, 1, 3).reshape(9 * channels, 3 * channels)
    hidden = depth_sum(
        jnp.dot(columns, weight_fwd, preferred_element_type=jnp.float32),
        extent_z,
        channels,
        False,
    )
    gate_sig = jax.nn.sigmoid(hidden)
    activation = (hidden * gate_sig).astype(jnp.bfloat16)
    tokens_in = to_tokens(activation.reshape(extent_x, extent_y, extent_z, channels))
    tok_count = tokens_in.shape[0]
    trunk_rows = jnp.dot(tokens_in, down_weight, preferred_element_type=jnp.float32)
    mean_rows = jnp.mean(trunk_rows, axis=-1, keepdims=True)
    centred = trunk_rows - mean_rows
    inverse_std = lax.rsqrt(jnp.mean(centred * centred, axis=-1, keepdims=True) + 1e-05)
    normed = centred * inverse_std
    normed_b = (normed * norm_gain).astype(jnp.bfloat16)
    qkv_rows = jnp.dot(normed_b, qkv_weight, preferred_element_type=jnp.float32).astype(
        jnp.bfloat16
    )
    queries = qkv_rows[:, :model_width]
    local_keys = qkv_rows[:, model_width : 2 * model_width]
    local_values = qkv_rows[:, 2 * model_width :]
    gathered = lax.all_gather(
        qkv_rows[:, model_width:], ("gx", "gy"), axis=0, tiled=True
    )
    all_keys = gathered[:, :model_width]
    all_values = gathered[:, model_width:]
    queries_h = queries.reshape(tok_count, H, HD)
    keys_h = all_keys.reshape(-1, H, HD)
    values_h = all_values.reshape(-1, H, HD)
    scores = (
        jnp.einsum("ihe,jhe->hij", queries_h, keys_h, preferred_element_type=jnp.float32)
        * score_scale
    )
    exp_scores = jnp.exp(scores)
    totals = jnp.sum(exp_scores, axis=-1)
    attn_probs = exp_scores / totals[:, :, None]
    probs_b = attn_probs.astype(jnp.bfloat16)
    attended = jnp.einsum("hij,jhe->ihe", probs_b, values_h, preferred_element_type=jnp.float32)
    attended = attended.reshape(tok_count, model_width).astype(jnp.bfloat16)
    cotangent = upstream.reshape(tok_count, model_width)
    cot_float = cotangent.astype(jnp.float32)
    out_part = jnp.einsum("td,te->de", attended, cotangent, preferred_element_type=jnp.float32)
    d_attended = jnp.dot(cotangent, out_weight.T, preferred_element_type=jnp.float32).astype(
        jnp.bfloat16
    )
    d_att_h = d_attended.reshape(tok_count, H, HD)
    d_probs = jnp.einsum("ihe,jhe->hij", d_att_h, values_h, preferred_element_type=jnp.float32)
    d_probs = d_probs.astype(jnp.bfloat16).astype(jnp.float32)
    row_delta = jnp.sum(attn_probs * d_probs, axis=-1)
    d_scores = attn_probs * (d_probs - row_delta[:, :, None])
    d_queries = (
        jnp.einsum(
            "hij,jhe->ihe", d_scores, keys_h, precision=precise, preferred_element_type=jnp.float32
        )
        * score_scale
    )
    key_term = (
        jnp.einsum(
            "hij,ihe->jhe",
            d_scores,
            queries_h,
            precision=precise,
            preferred_element_type=jnp.float32,
        )
        * score_scale
    )
    value_term = jnp.einsum("hij,ihe->jhe", probs_b, d_att_h, preferred_element_type=jnp.float32)
    groups = lax.axis_size(("gx", "gy"))
    key_parts = jnp.concatenate(
        [
            key_term.reshape(tok_count * groups, model_width),
            value_term.reshape(tok_count * groups, model_width),
        ],
        axis=1,
    ).astype(jnp.bfloat16)
    key_parts = lax.all_to_all(key_parts, ("gx", "gy"), 0, 0, tiled=True)
    key_sums = jnp.sum(
        key_parts.reshape(groups, tok_count, 2 * model_width).astype(jnp.float32), axis=0
    )
    d_keys = key_sums[:, :model_width].astype(jnp.bfloat16)
    d_values = key_sums[:, model_width:].astype(jnp.bfloat16)
    d_qkv = jnp.concatenate(
        [d_queries.reshape(tok_count, model_width).astype(jnp.bfloat16), d_keys, d_values], axis=1
    )
    qkv_part = jnp.einsum("td,te->de", normed_b, d_qkv, preferred_element_type=jnp.float32)
    d_normed = (
        jnp.dot(d_qkv, qkv_weight.T, preferred_element_type=jnp.float32)
        .astype(jnp.bfloat16)
        .astype(jnp.float32)
    )
    d_hat = d_normed * norm_gain
    gain_part = jnp.sum(d_normed * normed, axis=0)
    d_trunk = cot_float + inverse_std * (
        d_hat
        - jnp.mean(d_hat, axis=-1, keepdims=True)
        - normed * jnp.mean(d_hat * normed, axis=-1, keepdims=True)
    )
    down_part = jnp.einsum(
        "tr,td->rd", tokens_in, d_trunk, precision=precise, preferred_element_type=jnp.float32
    )
    d_activation = jnp.dot(
        d_trunk, down_weight.T, precision=precise, preferred_element_type=jnp.float32
    ).astype(jnp.bfloat16)
    d_act_grid = lax.optimization_barrier(
        from_tokens(d_activation, extent_x, extent_y, extent_z).reshape(voxels, channels)
    ).astype(jnp.float32)
    d_hidden = (d_act_grid * gate_sig * (1.0 + hidden * (1.0 - gate_sig))).astype(jnp.bfloat16)
    d_depth = d_hidden.reshape(-1, extent_z, channels)
    d_shifts = [
        jnp.pad(d_depth[:, 1:], ((0, 0), (0, 1), (0, 0))),
        d_depth,
        jnp.pad(d_depth[:, :-1], ((0, 0), (1, 0), (0, 0))),
    ]
    conv_blocks = [
        jnp.einsum(
            "vr,vc->rc",
            columns,
            shifted.reshape(voxels, channels),
            preferred_element_type=jnp.float32,
        )
        .astype(jnp.bfloat16)
        .reshape(9, channels, channels)
        for shifted in d_shifts
    ]
    conv_part = jnp.stack(conv_blocks, axis=1).reshape(27 * channels, channels)
    d_padded = padded_2(
        d_hidden.reshape(extent_x, extent_y, extent_z, channels), (("gx", 0), ("gy", 1)), 1
    )
    d_columns = plane_columns(d_padded, extent_x, extent_y, True)
    weight_bwd = taps.transpose(0, 3, 1, 2).reshape(9 * channels, 3 * channels)
    grad_features = depth_sum(
        jnp.dot(d_columns, weight_bwd, preferred_element_type=jnp.float32),
        extent_z,
        channels,
        True,
    )
    grad_features = grad_features.reshape(extent_x, extent_y, extent_z, channels).astype(
        jnp.bfloat16
    )
    groups = lax.axis_size(("gx", "gy"))
    gain_rows = gain_part.reshape(groups, -1)
    gain_high = gain_rows.astype(jnp.bfloat16)
    gain_low = (gain_rows - gain_high.astype(jnp.float32)).astype(jnp.bfloat16)
    gain_pair = jnp.concatenate([gain_high, gain_low], axis=1)
    gain_pair = jnp.pad(gain_pair, ((0, 0), (0, 4096 - gain_pair.shape[1])))
    pieces = [
        down_part.astype(jnp.bfloat16),
        qkv_part.astype(jnp.bfloat16),
        out_part.astype(jnp.bfloat16),
    ]
    shapes = [piece.shape for piece in pieces]
    flat = [piece.reshape(groups, -1, 512) for piece in pieces] + [gain_pair.reshape(groups, -1, 512)]
    heights = [piece.shape[1] for piece in flat]
    joined = jnp.concatenate(flat, axis=1)
    summed = lax.psum_scatter(
        joined.reshape(-1, 512), ("gx", "gy"), scatter_dimension=0, tiled=True
    )
    summed = lax.optimization_barrier(summed)
    results = []
    offset = 0
    for height in heights:
        results.append(summed[offset : offset + height])
        offset += height
    down_sum, qkv_sum, out_sum = [
        piece.reshape(shape[0] // groups, shape[1]) for piece, shape in zip(results[:3], shapes)
    ]
    conv_rows = lax.all_to_all(conv_part, ("gx", "gy"), 0, 0, tiled=True)
    conv_sum = jnp.sum(
        conv_rows.reshape(groups, -1, channels).astype(jnp.float32), axis=0
    )
    gain_flat = results[3].reshape(-1).astype(jnp.float32)
    half = gain_high.shape[1]
    gain_sum = gain_flat[:half] + gain_flat[half : 2 * half]
    return (
        grad_features,
        conv_sum.astype(jnp.bfloat16),
        down_sum.astype(jnp.bfloat16),
        gain_sum,
        qkv_sum.astype(jnp.bfloat16),
        out_sum.astype(jnp.bfloat16),
    )


def solution(mesh):
    placed = (
        P(("batch", "gx"), "gy", None, None),
        P(),
        P(),
        P(),
        P(),
        P(),
        P(("batch", "gx"), "gy", None, None),
    )
    return jax.shard_map(
        local,
        mesh=mesh,
        in_specs=placed,
        out_specs=(
            P(("batch", "gx"), "gy", None, None),
            P(("batch", "gx", "gy"), None),
            P(("batch", "gx", "gy"), None),
            P(("batch", "gx", "gy")),
            P(("batch", "gx", "gy"), None),
            P(("batch", "gx", "gy"), None),
        ),
        check_vma=False,
    )
```

```python
import jax
import jax.numpy as jnp
from jax import lax
from jax.sharding import PartitionSpec as P

H = 8
HD = 64


precise = lax.Precision.HIGHEST


def padded_2(block, sides):
    for axis, dim, width in sides:
        count = lax.axis_size(axis)
        forward = [(i, i + 1) for i in range(count - 1)]
        backward = [(target, source) for source, target in forward]
        low = lax.ppermute(
            lax.slice_in_dim(block, block.shape[dim] - width, None, axis=dim), axis, forward
        )
        high = lax.ppermute(lax.slice_in_dim(block, 0, width, axis=dim), axis, backward)
        block = jnp.concatenate([low, block, high], axis=dim)
    return block


def to_tokens(volume):
    extent_x, extent_y, extent_z, channels = volume.shape
    grid = volume.reshape(extent_x // 2, 2, extent_y // 2, 2, extent_z // 2, 2, channels)
    grid = grid.transpose(0, 2, 4, 1, 3, 5, 6)
    return grid.reshape(extent_x * extent_y * extent_z // 8, 8 * channels)


def from_tokens(matrix, extent_x, extent_y, extent_z):
    channels = matrix.shape[1] // 8
    grid = matrix.reshape(extent_x // 2, extent_y // 2, extent_z // 2, 2, 2, 2, channels)
    grid = grid.transpose(0, 3, 1, 4, 2, 5, 6)
    return grid.reshape(extent_x, extent_y, extent_z, channels)


def plane_columns(padded, extent_x, extent_y, extent_z, flipped):
    channels = padded.shape[2]
    rows = extent_x * extent_y * extent_z
    pieces = []
    for offset_x in range(3):
        for offset_y in range(3):
            start_x = 2 - offset_x if flipped else offset_x
            start_y = 2 - offset_y if flipped else offset_y
            pieces.append(
                padded[
                    start_x : start_x + extent_x,
                    start_y * extent_z : (start_y + extent_y) * extent_z,
                ].reshape(rows, channels)
            )
    return jnp.concatenate(pieces, axis=1)


def depth_sum(product, extent_z, channels, flipped):
    grid = product.reshape(-1, extent_z, 3, channels)
    first, last = (2, 0) if flipped else (0, 2)
    below = jnp.pad(grid[:, :-1, first], ((0, 0), (1, 0), (0, 0)))
    above = jnp.pad(grid[:, 1:, last], ((0, 0), (0, 1), (0, 0)))
    return (below + grid[:, :, 1] + above).reshape(-1, channels)


def local(features, conv_weight, down_weight, norm_gain, qkv_weight, out_weight, upstream):
    extent_x, extent_y, extent_z, channels = features.shape
    model_width = out_weight.shape[0]
    voxels = extent_x * extent_y * extent_z
    score_scale = HD ** (-0.5)
    taps = conv_weight.reshape(9, 3, channels, channels)
    flat_features = features.reshape(extent_x, extent_y * extent_z, channels)
    padded = padded_2(flat_features, (("gx", 0, 1), ("gy", 1, extent_z)))
    columns = plane_columns(padded, extent_x, extent_y, extent_z, False)
    weight_fwd = taps.transpose(0, 2, 1, 3).reshape(9 * channels, 3 * channels)
    hidden = depth_sum(
        jnp.dot(columns, weight_fwd, preferred_element_type=jnp.float32),
        extent_z,
        channels,
        False,
    )
    gate_sig = jax.nn.sigmoid(hidden)
    activation = (hidden * gate_sig).astype(jnp.bfloat16)
    tokens_in = to_tokens(activation.reshape(extent_x, extent_y, extent_z, channels))
    tok_count = tokens_in.shape[0]
    trunk_rows = jnp.dot(tokens_in, down_weight, preferred_element_type=jnp.float32)
    mean_rows = jnp.mean(trunk_rows, axis=-1, keepdims=True)
    centred = trunk_rows - mean_rows
    inverse_std = lax.rsqrt(jnp.mean(centred * centred, axis=-1, keepdims=True) + 1e-05)
    normed = centred * inverse_std
    normed_b = (normed * norm_gain).astype(jnp.bfloat16)
    qkv_rows = jnp.dot(normed_b, qkv_weight, preferred_element_type=jnp.float32).astype(
        jnp.bfloat16
    )
    queries = qkv_rows[:, :model_width]
    local_keys = qkv_rows[:, model_width : 2 * model_width]
    local_values = qkv_rows[:, 2 * model_width :]
    gathered = lax.all_gather(
        qkv_rows[:, model_width:], ("gx", "gy"), axis=0, tiled=True
    )
    all_keys = gathered[:, :model_width]
    all_values = gathered[:, model_width:]
    queries_h = queries.reshape(tok_count, H, HD)
    keys_h = all_keys.reshape(-1, H, HD)
    values_h = all_values.reshape(-1, H, HD)
    scores = (
        jnp.einsum("ihe,jhe->hij", queries_h, keys_h, preferred_element_type=jnp.float32)
        * score_scale
    )
    exp_scores = jnp.exp(scores)
    totals = jnp.sum(exp_scores, axis=-1)
    attn_probs = exp_scores / totals[:, :, None]
    probs_b = attn_probs.astype(jnp.bfloat16)
    attended = jnp.einsum("hij,jhe->ihe", probs_b, values_h, preferred_element_type=jnp.float32)
    attended = attended.reshape(tok_count, model_width).astype(jnp.bfloat16)
    cotangent = upstream.reshape(tok_count, model_width)
    cot_float = cotangent.astype(jnp.float32)
    out_part = jnp.einsum("td,te->de", attended, cotangent, preferred_element_type=jnp.float32)
    d_attended = jnp.dot(cotangent, out_weight.T, preferred_element_type=jnp.float32).astype(
        jnp.bfloat16
    )
    d_att_h = d_attended.reshape(tok_count, H, HD)
    d_probs = jnp.einsum("ihe,jhe->hij", d_att_h, values_h, preferred_element_type=jnp.float32)
    d_probs = d_probs.astype(jnp.bfloat16).astype(jnp.float32)
    row_delta = jnp.sum(attn_probs * d_probs, axis=-1)
    d_scores = attn_probs * (d_probs - row_delta[:, :, None])
    d_queries = (
        jnp.einsum(
            "hij,jhe->ihe", d_scores, keys_h, precision=precise, preferred_element_type=jnp.float32
        )
        * score_scale
    )
    key_term = (
        jnp.einsum(
            "hij,ihe->jhe",
            d_scores,
            queries_h,
            precision=precise,
            preferred_element_type=jnp.float32,
        )
        * score_scale
    )
    value_term = jnp.einsum("hij,ihe->jhe", probs_b, d_att_h, preferred_element_type=jnp.float32)
    groups = lax.axis_size(("gx", "gy"))
    key_parts = jnp.concatenate(
        [
            key_term.reshape(tok_count * groups, model_width),
            value_term.reshape(tok_count * groups, model_width),
        ],
        axis=1,
    ).astype(jnp.bfloat16)
    key_parts = lax.all_to_all(key_parts, ("gx", "gy"), 0, 0, tiled=True)
    key_sums = jnp.sum(
        key_parts.reshape(groups, tok_count, 2 * model_width).astype(jnp.float32), axis=0
    )
    d_keys = key_sums[:, :model_width].astype(jnp.bfloat16)
    d_values = key_sums[:, model_width:].astype(jnp.bfloat16)
    d_qkv = jnp.concatenate(
        [d_queries.reshape(tok_count, model_width).astype(jnp.bfloat16), d_keys, d_values], axis=1
    )
    qkv_part = jnp.einsum("td,te->de", normed_b, d_qkv, preferred_element_type=jnp.float32)
    d_normed = (
        jnp.dot(d_qkv, qkv_weight.T, preferred_element_type=jnp.float32)
        .astype(jnp.bfloat16)
        .astype(jnp.float32)
    )
    d_hat = d_normed * norm_gain
    gain_part = jnp.sum(d_normed * normed, axis=0)
    d_trunk = cot_float + inverse_std * (
        d_hat
        - jnp.mean(d_hat, axis=-1, keepdims=True)
        - normed * jnp.mean(d_hat * normed, axis=-1, keepdims=True)
    )
    down_part = jnp.einsum(
        "tr,td->rd", tokens_in, d_trunk, precision=precise, preferred_element_type=jnp.float32
    )
    d_activation = jnp.dot(
        d_trunk, down_weight.T, precision=precise, preferred_element_type=jnp.float32
    ).astype(jnp.bfloat16)
    d_act_grid = (
        from_tokens(d_activation, extent_x, extent_y, extent_z)
        .reshape(voxels, channels)
        .astype(jnp.float32)
    )
    d_hidden = (d_act_grid * gate_sig * (1.0 + hidden * (1.0 - gate_sig))).astype(jnp.bfloat16)
    d_depth = d_hidden.reshape(-1, extent_z, channels)
    d_shifts = [
        jnp.pad(d_depth[:, 1:], ((0, 0), (0, 1), (0, 0))),
        d_depth,
        jnp.pad(d_depth[:, :-1], ((0, 0), (1, 0), (0, 0))),
    ]
    conv_blocks = [
        jnp.einsum(
            "vr,vc->rc",
            columns,
            shifted.reshape(voxels, channels),
            preferred_element_type=jnp.float32,
        )
        .astype(jnp.bfloat16)
        .reshape(9, channels, channels)
        for shifted in d_shifts
    ]
    conv_part = jnp.stack(conv_blocks, axis=1).reshape(27 * channels, channels)
    d_padded = padded_2(
        d_hidden.reshape(extent_x, extent_y * extent_z, channels),
        (("gx", 0, 1), ("gy", 1, extent_z)),
    )
    d_columns = plane_columns(d_padded, extent_x, extent_y, extent_z, True)
    weight_bwd = taps.transpose(0, 3, 1, 2).reshape(9 * channels, 3 * channels)
    grad_features = depth_sum(
        jnp.dot(d_columns, weight_bwd, preferred_element_type=jnp.float32),
        extent_z,
        channels,
        True,
    )
    grad_features = grad_features.reshape(extent_x, extent_y, extent_z, channels).astype(
        jnp.bfloat16
    )
    groups = lax.axis_size(("gx", "gy"))
    gain_rows = gain_part.reshape(groups, -1)
    gain_high = gain_rows.astype(jnp.bfloat16)
    gain_low = (gain_rows - gain_high.astype(jnp.float32)).astype(jnp.bfloat16)
    gain_pair = jnp.concatenate([gain_high, gain_low], axis=1)
    gain_pair = jnp.pad(gain_pair, ((0, 0), (0, 1024 - gain_pair.shape[1])))
    pieces = [
        down_part.astype(jnp.bfloat16),
        qkv_part.astype(jnp.bfloat16),
        out_part.astype(jnp.bfloat16),
    ]
    shapes = [piece.shape for piece in pieces]
    flat = [piece.reshape(groups, -1, 128) for piece in pieces] + [gain_pair.reshape(groups, -1, 128)]
    heights = [piece.shape[1] for piece in flat]
    joined = jnp.concatenate(flat, axis=1)
    summed = lax.psum_scatter(
        joined.reshape(-1, 128), ("gx", "gy"), scatter_dimension=0, tiled=True
    )
    summed = lax.optimization_barrier(summed)
    results = []
    offset = 0
    for height in heights:
        results.append(summed[offset : offset + height])
        offset += height
    down_sum, qkv_sum, out_sum = [
        piece.reshape(shape[0] // groups, shape[1]) for piece, shape in zip(results[:3], shapes)
    ]
    conv_rows = lax.all_to_all(conv_part, ("gx", "gy"), 0, 0, tiled=True)
    conv_sum = jnp.sum(
        conv_rows.reshape(groups, -1, channels).astype(jnp.float32), axis=0
    )
    gain_flat = results[3].reshape(-1).astype(jnp.float32)
    half = gain_high.shape[1]
    gain_sum = gain_flat[:half] + gain_flat[half : 2 * half]
    return (
        grad_features,
        conv_sum.astype(jnp.bfloat16),
        down_sum.astype(jnp.bfloat16),
        gain_sum,
        qkv_sum.astype(jnp.bfloat16),
        out_sum.astype(jnp.bfloat16),
    )


def solution(mesh):
    placed = (
        P(("batch", "gx"), "gy", None, None),
        P(),
        P(),
        P(),
        P(),
        P(),
        P(("batch", "gx"), "gy", None, None),
    )
    return jax.shard_map(
        local,
        mesh=mesh,
        in_specs=placed,
        out_specs=(
            P(("batch", "gx"), "gy", None, None),
            P(("batch", "gx", "gy"), None),
            P(("batch", "gx", "gy"), None),
            P(("batch", "gx", "gy")),
            P(("batch", "gx", "gy"), None),
            P(("batch", "gx", "gy"), None),
        ),
        check_vma=False,
    )
```

```python
import jax
import jax.numpy as jnp
from jax import lax
from jax.sharding import PartitionSpec as P

H = 8
HD = 64


precise = lax.Precision.HIGHEST


def padded_2(block, sides, width):
    (axis_x, dim_x), (axis_y, dim_y) = sides
    count_x = lax.axis_size(axis_x)
    count_y = lax.axis_size(axis_y)
    extent_x = block.shape[dim_x]
    extent_y = block.shape[dim_y]
    edges = {
        -1: (extent_x - width, extent_x),
        0: (0, extent_x),
        1: (0, width),
    }
    edges_y = {
        -1: (extent_y - width, extent_y),
        0: (0, extent_y),
        1: (0, width),
    }
    received = {}
    for offset_x in (-1, 0, 1):
        for offset_y in (-1, 0, 1):
            if offset_x == 0 and offset_y == 0:
                continue
            piece = lax.slice_in_dim(block, *edges[offset_x], axis=dim_x)
            piece = lax.slice_in_dim(piece, *edges_y[offset_y], axis=dim_y)
            pairs = []
            for source_x in range(count_x):
                for source_y in range(count_y):
                    target_x = source_x - offset_x
                    target_y = source_y - offset_y
                    if 0 <= target_x < count_x and 0 <= target_y < count_y:
                        pairs.append(
                            (source_x * count_y + source_y, target_x * count_y + target_y)
                        )
            received[offset_x, offset_y] = lax.ppermute(piece, (axis_x, axis_y), pairs)
    received[0, 0] = block
    rows = [
        jnp.concatenate([received[offset_x, offset_y] for offset_y in (-1, 0, 1)], axis=dim_y)
        for offset_x in (-1, 0, 1)
    ]
    return jnp.concatenate(rows, axis=dim_x)


def to_tokens(volume):
    extent_x, extent_y, extent_z, channels = volume.shape
    grid = volume.reshape(extent_x // 2, 2, extent_y // 2, 2, extent_z // 2, 2, channels)
    grid = grid.transpose(0, 2, 4, 1, 3, 5, 6)
    return grid.reshape(extent_x * extent_y * extent_z // 8, 8 * channels)


def from_tokens(matrix, extent_x, extent_y, extent_z):
    channels = matrix.shape[1] // 8
    grid = matrix.reshape(extent_x // 2, extent_y // 2, extent_z // 2, 2, 2, 2, channels)
    grid = grid.transpose(0, 3, 1, 4, 2, 5, 6)
    return grid.reshape(extent_x, extent_y, extent_z, channels)


def plane_columns(padded, extent_x, extent_y, flipped):
    channels = padded.shape[3]
    rows = extent_x * extent_y * padded.shape[2]
    pieces = []
    for offset_x in range(3):
        for offset_y in range(3):
            start_x = 2 - offset_x if flipped else offset_x
            start_y = 2 - offset_y if flipped else offset_y
            pieces.append(
                padded[start_x : start_x + extent_x, start_y : start_y + extent_y].reshape(
                    rows, channels
                )
            )
    return jnp.concatenate(pieces, axis=1)


def depth_sum(product, extent_z, channels, flipped):
    grid = product.reshape(-1, extent_z, 3, channels)
    first, last = (2, 0) if flipped else (0, 2)
    below = jnp.pad(grid[:, :-1, first], ((0, 0), (1, 0), (0, 0)))
    above = jnp.pad(grid[:, 1:, last], ((0, 0), (0, 1), (0, 0)))
    return (below + grid[:, :, 1] + above).reshape(-1, channels)


def local(features, conv_weight, down_weight, norm_gain, qkv_weight, out_weight, upstream):
    extent_x, extent_y, extent_z, channels = features.shape
    model_width = out_weight.shape[0]
    voxels = extent_x * extent_y * extent_z
    score_scale = HD ** (-0.5)
    taps = conv_weight.reshape(9, 3, channels, channels)
    padded = padded_2(features, (("gx", 0), ("gy", 1)), 1)
    columns = plane_columns(padded, extent_x, extent_y, False)
    weight_fwd = taps.transpose(0, 2, 1, 3).reshape(9 * channels, 3 * channels)
    hidden = depth_sum(
        jnp.dot(columns, weight_fwd, preferred_element_type=jnp.float32),
        extent_z,
        channels,
        False,
    )
    gate_sig = jax.nn.sigmoid(hidden)
    activation = (hidden * gate_sig).astype(jnp.bfloat16)
    tokens_in = to_tokens(activation.reshape(extent_x, extent_y, extent_z, channels))
    tok_count = tokens_in.shape[0]
    trunk_rows = jnp.dot(tokens_in, down_weight, preferred_element_type=jnp.float32)
    mean_rows = jnp.mean(trunk_rows, axis=-1, keepdims=True)
    centred = trunk_rows - mean_rows
    inverse_std = lax.rsqrt(jnp.mean(centred * centred, axis=-1, keepdims=True) + 1e-05)
    normed = centred * inverse_std
    normed_b = (normed * norm_gain).astype(jnp.bfloat16)
    qkv_rows = jnp.dot(normed_b, qkv_weight, preferred_element_type=jnp.float32).astype(
        jnp.bfloat16
    )
    queries = qkv_rows[:, :model_width]
    local_keys = qkv_rows[:, model_width : 2 * model_width]
    local_values = qkv_rows[:, 2 * model_width :]
    gathered = lax.all_gather(
        qkv_rows[:, model_width:], ("gx", "gy"), axis=0, tiled=True
    )
    all_keys = gathered[:, :model_width]
    all_values = gathered[:, model_width:]
    queries_h = queries.reshape(tok_count, H, HD)
    keys_h = all_keys.reshape(-1, H, HD)
    values_h = all_values.reshape(-1, H, HD)
    scores = (
        jnp.einsum("ihe,jhe->hij", queries_h, keys_h, preferred_element_type=jnp.float32)
        * score_scale
    )
    exp_scores = jnp.exp(scores)
    totals = jnp.sum(exp_scores, axis=-1)
    attn_probs = exp_scores / totals[:, :, None]
    probs_b = attn_probs.astype(jnp.bfloat16)
    attended = jnp.einsum("hij,jhe->ihe", probs_b, values_h, preferred_element_type=jnp.float32)
    attended = attended.reshape(tok_count, model_width).astype(jnp.bfloat16)
    cotangent = upstream.reshape(tok_count, model_width)
    cot_float = cotangent.astype(jnp.float32)
    out_part = jnp.einsum("td,te->de", attended, cotangent, preferred_element_type=jnp.float32)
    d_attended = jnp.dot(cotangent, out_weight.T, preferred_element_type=jnp.float32).astype(
        jnp.bfloat16
    )
    d_att_h = d_attended.reshape(tok_count, H, HD)
    d_probs = jnp.einsum("ihe,jhe->hij", d_att_h, values_h, preferred_element_type=jnp.float32)
    d_probs = d_probs.astype(jnp.bfloat16).astype(jnp.float32)
    row_delta = jnp.sum(attn_probs * d_probs, axis=-1)
    d_scores = attn_probs * (d_probs - row_delta[:, :, None])
    d_queries = (
        jnp.einsum(
            "hij,jhe->ihe", d_scores, keys_h, precision=precise, preferred_element_type=jnp.float32
        )
        * score_scale
    )
    key_term = (
        jnp.einsum(
            "hij,ihe->jhe",
            d_scores,
            queries_h,
            precision=precise,
            preferred_element_type=jnp.float32,
        )
        * score_scale
    )
    value_term = jnp.einsum("hij,ihe->jhe", probs_b, d_att_h, preferred_element_type=jnp.float32)
    groups = lax.axis_size(("gx", "gy"))
    key_parts = jnp.concatenate(
        [
            key_term.reshape(tok_count * groups, model_width),
            value_term.reshape(tok_count * groups, model_width),
        ],
        axis=1,
    ).astype(jnp.bfloat16)
    key_parts = lax.all_to_all(key_parts, ("gx", "gy"), 0, 0, tiled=True)
    key_sums = jnp.sum(
        key_parts.reshape(groups, tok_count, 2 * model_width).astype(jnp.float32), axis=0
    )
    d_keys = key_sums[:, :model_width].astype(jnp.bfloat16)
    d_values = key_sums[:, model_width:].astype(jnp.bfloat16)
    d_qkv = jnp.concatenate(
        [d_queries.reshape(tok_count, model_width).astype(jnp.bfloat16), d_keys, d_values], axis=1
    )
    qkv_part = jnp.einsum("td,te->de", normed_b, d_qkv, preferred_element_type=jnp.float32)
    d_normed = (
        jnp.dot(d_qkv, qkv_weight.T, preferred_element_type=jnp.float32)
        .astype(jnp.bfloat16)
        .astype(jnp.float32)
    )
    d_hat = d_normed * norm_gain
    gain_part = jnp.sum(d_normed * normed, axis=0)
    d_trunk = cot_float + inverse_std * (
        d_hat
        - jnp.mean(d_hat, axis=-1, keepdims=True)
        - normed * jnp.mean(d_hat * normed, axis=-1, keepdims=True)
    )
    down_part = jnp.einsum(
        "tr,td->rd", tokens_in, d_trunk, precision=precise, preferred_element_type=jnp.float32
    )
    d_activation = jnp.dot(
        d_trunk, down_weight.T, precision=precise, preferred_element_type=jnp.float32
    ).astype(jnp.bfloat16)
    d_act_grid = (
        from_tokens(d_activation, extent_x, extent_y, extent_z)
        .reshape(voxels, channels)
        .astype(jnp.float32)
    )
    d_hidden = (d_act_grid * gate_sig * (1.0 + hidden * (1.0 - gate_sig))).astype(jnp.bfloat16)
    d_depth = d_hidden.reshape(-1, extent_z, channels)
    d_shifts = [
        jnp.pad(d_depth[:, 1:], ((0, 0), (0, 1), (0, 0))),
        d_depth,
        jnp.pad(d_depth[:, :-1], ((0, 0), (1, 0), (0, 0))),
    ]
    conv_blocks = [
        jnp.einsum(
            "vr,vc->rc",
            columns,
            shifted.reshape(voxels, channels),
            preferred_element_type=jnp.float32,
        )
        .astype(jnp.bfloat16)
        .reshape(9, channels, channels)
        for shifted in d_shifts
    ]
    conv_part = jnp.stack(conv_blocks, axis=1).reshape(27 * channels, channels)
    d_padded = padded_2(
        d_hidden.reshape(extent_x, extent_y, extent_z, channels), (("gx", 0), ("gy", 1)), 1
    )
    d_columns = plane_columns(d_padded, extent_x, extent_y, True)
    weight_bwd = taps.transpose(0, 3, 1, 2).reshape(9 * channels, 3 * channels)
    grad_features = depth_sum(
        jnp.dot(d_columns, weight_bwd, preferred_element_type=jnp.float32),
        extent_z,
        channels,
        True,
    )
    grad_features = grad_features.reshape(extent_x, extent_y, extent_z, channels).astype(
        jnp.bfloat16
    )
    groups = lax.axis_size(("gx", "gy"))
    gain_rows = gain_part.reshape(groups, -1)
    gain_high = gain_rows.astype(jnp.bfloat16)
    gain_low = (gain_rows - gain_high.astype(jnp.float32)).astype(jnp.bfloat16)
    gain_pair = jnp.concatenate([gain_high, gain_low], axis=1)
    gain_pair = jnp.pad(gain_pair, ((0, 0), (0, 1024 - gain_pair.shape[1])))
    pieces = [
        down_part.astype(jnp.bfloat16),
        qkv_part.astype(jnp.bfloat16),
        out_part.astype(jnp.bfloat16),
    ]
    shapes = [piece.shape for piece in pieces]
    flat = [piece.reshape(groups, -1, 128) for piece in pieces] + [gain_pair.reshape(groups, -1, 128)]
    heights = [piece.shape[1] for piece in flat]
    joined = jnp.concatenate(flat, axis=1)
    summed = lax.psum_scatter(
        joined.reshape(-1, 128), ("gx", "gy"), scatter_dimension=0, tiled=True
    )
    summed = lax.optimization_barrier(summed)
    results = []
    offset = 0
    for height in heights:
        results.append(summed[offset : offset + height])
        offset += height
    down_sum, qkv_sum, out_sum = [
        piece.reshape(shape[0] // groups, shape[1]) for piece, shape in zip(results[:3], shapes)
    ]
    conv_rows = lax.all_to_all(conv_part, ("gx", "gy"), 0, 0, tiled=True)
    conv_sum = jnp.sum(
        conv_rows.reshape(groups, -1, channels).astype(jnp.float32), axis=0
    )
    gain_flat = results[3].reshape(-1).astype(jnp.float32)
    half = gain_high.shape[1]
    gain_sum = gain_flat[:half] + gain_flat[half : 2 * half]
    return (
        grad_features,
        conv_sum.astype(jnp.bfloat16),
        down_sum.astype(jnp.bfloat16),
        gain_sum,
        qkv_sum.astype(jnp.bfloat16),
        out_sum.astype(jnp.bfloat16),
    )


def solution(mesh):
    placed = (
        P(("batch", "gx"), "gy", None, None),
        P(),
        P(),
        P(),
        P(),
        P(),
        P(("batch", "gx"), "gy", None, None),
    )
    return jax.shard_map(
        local,
        mesh=mesh,
        in_specs=placed,
        out_specs=(
            P(("batch", "gx"), "gy", None, None),
            P(("batch", "gx", "gy"), None),
            P(("batch", "gx", "gy"), None),
            P(("batch", "gx", "gy")),
            P(("batch", "gx", "gy"), None),
            P(("batch", "gx", "gy"), None),
        ),
        check_vma=False,
    )
```

```python
import jax
import jax.numpy as jnp
from jax import lax
from jax.sharding import PartitionSpec as P

H = 8
HD = 64


precise = lax.Precision.HIGHEST


def padded_2(block, sides, width):
    for axis, dim in sides:
        count = lax.axis_size(axis)
        forward = [(i, i + 1) for i in range(count - 1)]
        backward = [(target, source) for source, target in forward]
        low = lax.ppermute(
            lax.slice_in_dim(block, block.shape[dim] - width, None, axis=dim), axis, forward
        )
        high = lax.ppermute(lax.slice_in_dim(block, 0, width, axis=dim), axis, backward)
        block = jnp.concatenate([low, block, high], axis=dim)
    return block


def to_tokens(volume):
    extent_x, extent_y, extent_z, channels = volume.shape
    grid = volume.reshape(extent_x // 2, 2, extent_y // 2, 2, extent_z // 2, 2, channels)
    grid = grid.transpose(0, 2, 4, 1, 3, 5, 6)
    return grid.reshape(extent_x * extent_y * extent_z // 8, 8 * channels)


def from_tokens(matrix, extent_x, extent_y, extent_z):
    channels = matrix.shape[1] // 8
    grid = matrix.reshape(extent_x // 2, extent_y // 2, extent_z // 2, 2, 2, 2, channels)
    grid = grid.transpose(0, 3, 1, 4, 2, 5, 6)
    return grid.reshape(extent_x, extent_y, extent_z, channels)


def plane_columns(padded, extent_x, extent_y, flipped):
    channels = padded.shape[3]
    rows = extent_x * extent_y * padded.shape[2]
    pieces = []
    for offset_x in range(3):
        for offset_y in range(3):
            start_x = 2 - offset_x if flipped else offset_x
            start_y = 2 - offset_y if flipped else offset_y
            pieces.append(
                padded[start_x : start_x + extent_x, start_y : start_y + extent_y].reshape(
                    rows, channels
                )
            )
    return jnp.concatenate(pieces, axis=1)


def depth_sum(product, extent_z, channels, flipped):
    grid = product.reshape(-1, extent_z, 3, channels)
    first, last = (2, 0) if flipped else (0, 2)
    below = jnp.pad(grid[:, :-1, first], ((0, 0), (1, 0), (0, 0)))
    above = jnp.pad(grid[:, 1:, last], ((0, 0), (0, 1), (0, 0)))
    return (below + grid[:, :, 1] + above).reshape(-1, channels)


def local(features, conv_weight, down_weight, norm_gain, qkv_weight, out_weight, upstream):
    extent_x, extent_y, extent_z, channels = features.shape
    model_width = out_weight.shape[0]
    voxels = extent_x * extent_y * extent_z
    score_scale = HD ** (-0.5)
    taps = conv_weight.reshape(9, 3, channels, channels)
    padded = padded_2(features, (("gx", 0), ("gy", 1)), 1)
    columns = plane_columns(padded, extent_x, extent_y, False)
    weight_fwd = taps.transpose(0, 2, 1, 3).reshape(9 * channels, 3 * channels)
    hidden = depth_sum(
        jnp.dot(columns, weight_fwd, preferred_element_type=jnp.float32),
        extent_z,
        channels,
        False,
    )
    gate_sig = jax.nn.sigmoid(hidden)
    activation = (hidden * gate_sig).astype(jnp.bfloat16)
    tokens_in = to_tokens(activation.reshape(extent_x, extent_y, extent_z, channels))
    tok_count = tokens_in.shape[0]
    trunk_rows = jnp.dot(tokens_in, down_weight, preferred_element_type=jnp.float32)
    mean_rows = jnp.mean(trunk_rows, axis=-1, keepdims=True)
    centred = trunk_rows - mean_rows
    inverse_std = lax.rsqrt(jnp.mean(centred * centred, axis=-1, keepdims=True) + 1e-05)
    normed = centred * inverse_std
    normed_b = (normed * norm_gain).astype(jnp.bfloat16)
    qkv_rows = jnp.dot(normed_b, qkv_weight, preferred_element_type=jnp.float32).astype(
        jnp.bfloat16
    )
    queries = qkv_rows[:, :model_width]
    local_keys = qkv_rows[:, model_width : 2 * model_width]
    local_values = qkv_rows[:, 2 * model_width :]
    gathered = lax.all_gather(
        qkv_rows[:, model_width:], ("gx", "gy"), axis=0, tiled=True
    )
    all_keys = gathered[:, :model_width]
    all_values = gathered[:, model_width:]
    queries_h = queries.reshape(tok_count, H, HD)
    keys_h = all_keys.reshape(-1, H, HD)
    values_h = all_values.reshape(-1, H, HD)
    scores = (
        jnp.einsum("ihe,jhe->hij", queries_h, keys_h, preferred_element_type=jnp.float32)
        * score_scale
    )
    exp_scores = jnp.exp(scores)
    totals = jnp.sum(exp_scores, axis=-1)
    attn_probs = exp_scores / totals[:, :, None]
    probs_b = attn_probs.astype(jnp.bfloat16)
    attended = jnp.einsum("hij,jhe->ihe", probs_b, values_h, preferred_element_type=jnp.float32)
    attended = attended.reshape(tok_count, model_width).astype(jnp.bfloat16)
    cotangent = upstream.reshape(tok_count, model_width)
    cot_float = cotangent.astype(jnp.float32)
    out_part = jnp.einsum("td,te->de", attended, cotangent, preferred_element_type=jnp.float32)
    d_attended = jnp.dot(cotangent, out_weight.T, preferred_element_type=jnp.float32).astype(
        jnp.bfloat16
    )
    d_att_h = d_attended.reshape(tok_count, H, HD)
    d_probs = jnp.einsum("ihe,jhe->hij", d_att_h, values_h, preferred_element_type=jnp.float32)
    d_probs = d_probs.astype(jnp.bfloat16).astype(jnp.float32)
    row_delta = jnp.sum(attn_probs * d_probs, axis=-1)
    d_scores = attn_probs * (d_probs - row_delta[:, :, None])
    d_queries = (
        jnp.einsum(
            "hij,jhe->ihe", d_scores, keys_h, precision=precise, preferred_element_type=jnp.float32
        )
        * score_scale
    )
    key_term = (
        jnp.einsum(
            "hij,ihe->jhe",
            d_scores,
            queries_h,
            precision=precise,
            preferred_element_type=jnp.float32,
        )
        * score_scale
    )
    value_term = jnp.einsum("hij,ihe->jhe", probs_b, d_att_h, preferred_element_type=jnp.float32)
    groups = lax.axis_size(("gx", "gy"))
    key_parts = jnp.concatenate(
        [
            key_term.reshape(tok_count * groups, model_width),
            value_term.reshape(tok_count * groups, model_width),
        ],
        axis=1,
    ).astype(jnp.bfloat16)
    key_parts = lax.all_to_all(key_parts, ("gx", "gy"), 0, 0, tiled=True)
    key_sums = jnp.sum(
        key_parts.reshape(groups, tok_count, 2 * model_width).astype(jnp.float32), axis=0
    )
    d_keys = key_sums[:, :model_width].astype(jnp.bfloat16)
    d_values = key_sums[:, model_width:].astype(jnp.bfloat16)
    d_qkv = jnp.concatenate(
        [d_queries.reshape(tok_count, model_width).astype(jnp.bfloat16), d_keys, d_values], axis=1
    )
    qkv_part = jnp.einsum("td,te->de", normed_b, d_qkv, preferred_element_type=jnp.float32)
    d_normed = (
        jnp.dot(d_qkv, qkv_weight.T, preferred_element_type=jnp.float32)
        .astype(jnp.bfloat16)
        .astype(jnp.float32)
    )
    d_hat = d_normed * norm_gain
    gain_part = jnp.sum(d_normed * normed, axis=0)
    d_trunk = cot_float + inverse_std * (
        d_hat
        - jnp.mean(d_hat, axis=-1, keepdims=True)
        - normed * jnp.mean(d_hat * normed, axis=-1, keepdims=True)
    )
    down_part = jnp.einsum(
        "tr,td->rd", tokens_in, d_trunk, precision=precise, preferred_element_type=jnp.float32
    )
    d_activation = jnp.dot(
        d_trunk, down_weight.T, precision=precise, preferred_element_type=jnp.float32
    ).astype(jnp.bfloat16)
    d_act_grid = (
        from_tokens(d_activation, extent_x, extent_y, extent_z)
        .reshape(voxels, channels)
        .astype(jnp.float32)
    )
    d_hidden = (d_act_grid * gate_sig * (1.0 + hidden * (1.0 - gate_sig))).astype(jnp.bfloat16)
    d_depth = d_hidden.reshape(-1, extent_z, channels)
    d_shifts = [
        jnp.pad(d_depth[:, 1:], ((0, 0), (0, 1), (0, 0))),
        d_depth,
        jnp.pad(d_depth[:, :-1], ((0, 0), (1, 0), (0, 0))),
    ]
    conv_blocks = [
        jnp.einsum(
            "vr,vc->rc",
            columns,
            shifted.reshape(voxels, channels),
            preferred_element_type=jnp.float32,
        )
        .astype(jnp.bfloat16)
        .reshape(9, channels, channels)
        for shifted in d_shifts
    ]
    conv_part = jnp.stack(conv_blocks, axis=1).reshape(27 * channels, channels)
    d_padded = padded_2(
        d_hidden.reshape(extent_x, extent_y, extent_z, channels), (("gx", 0), ("gy", 1)), 1
    )
    d_columns = plane_columns(d_padded, extent_x, extent_y, True)
    weight_bwd = taps.transpose(0, 3, 1, 2).reshape(9 * channels, 3 * channels)
    groups = lax.axis_size(("gx", "gy"))
    gain_rows = gain_part.reshape(groups, -1)
    gain_high = gain_rows.astype(jnp.bfloat16)
    gain_low = (gain_rows - gain_high.astype(jnp.float32)).astype(jnp.bfloat16)
    gain_pair = jnp.concatenate([gain_high, gain_low], axis=1)
    gain_pair = jnp.pad(gain_pair, ((0, 0), (0, 1024 - gain_pair.shape[1])))
    pieces = [
        down_part.astype(jnp.bfloat16),
        qkv_part.astype(jnp.bfloat16),
        out_part.astype(jnp.bfloat16),
    ]
    shapes = [piece.shape for piece in pieces]
    flat = [piece.reshape(groups, -1, 128) for piece in pieces] + [gain_pair.reshape(groups, -1, 128)]
    heights = [piece.shape[1] for piece in flat]
    joined = jnp.concatenate(flat, axis=1)
    summed = lax.psum_scatter(
        joined.reshape(-1, 128), ("gx", "gy"), scatter_dimension=0, tiled=True
    )
    summed = lax.optimization_barrier(summed)
    results = []
    offset = 0
    for height in heights:
        results.append(summed[offset : offset + height])
        offset += height
    down_sum, qkv_sum, out_sum = [
        piece.reshape(shape[0] // groups, shape[1]) for piece, shape in zip(results[:3], shapes)
    ]
    conv_rows = lax.all_to_all(conv_part, ("gx", "gy"), 0, 0, tiled=True)
    conv_sum = jnp.sum(
        conv_rows.reshape(groups, -1, channels).astype(jnp.float32), axis=0
    )
    gain_flat = results[3].reshape(-1).astype(jnp.float32)
    half = gain_high.shape[1]
    gain_sum = gain_flat[:half] + gain_flat[half : 2 * half]
    d_columns, down_sum, qkv_sum, out_sum, gain_sum = lax.optimization_barrier(
        (d_columns, down_sum, qkv_sum, out_sum, gain_sum)
    )
    grad_features = depth_sum(
        jnp.dot(d_columns, weight_bwd, preferred_element_type=jnp.float32),
        extent_z,
        channels,
        True,
    )
    grad_features = grad_features.reshape(extent_x, extent_y, extent_z, channels).astype(
        jnp.bfloat16
    )
    return (
        grad_features,
        conv_sum.astype(jnp.bfloat16),
        down_sum.astype(jnp.bfloat16),
        gain_sum,
        qkv_sum.astype(jnp.bfloat16),
        out_sum.astype(jnp.bfloat16),
    )


def solution(mesh):
    placed = (
        P(("batch", "gx"), "gy", None, None),
        P(),
        P(),
        P(),
        P(),
        P(),
        P(("batch", "gx"), "gy", None, None),
    )
    return jax.shard_map(
        local,
        mesh=mesh,
        in_specs=placed,
        out_specs=(
            P(("batch", "gx"), "gy", None, None),
            P(("batch", "gx", "gy"), None),
            P(("batch", "gx", "gy"), None),
            P(("batch", "gx", "gy")),
            P(("batch", "gx", "gy"), None),
            P(("batch", "gx", "gy"), None),
        ),
        check_vma=False,
    )
```

```python
import jax
import jax.numpy as jnp
from jax import lax
from jax.sharding import PartitionSpec as P

H = 8
HD = 64


precise = lax.Precision.HIGHEST


def padded_2(block, sides, width):
    for axis, dim in sides:
        count = lax.axis_size(axis)
        forward = [(i, i + 1) for i in range(count - 1)]
        backward = [(target, source) for source, target in forward]
        low = lax.ppermute(
            lax.slice_in_dim(block, block.shape[dim] - width, None, axis=dim), axis, forward
        )
        high = lax.ppermute(lax.slice_in_dim(block, 0, width, axis=dim), axis, backward)
        block = jnp.concatenate([low, block, high], axis=dim)
    return block


def to_tokens(volume):
    extent_x, extent_y, extent_z, channels = volume.shape
    grid = volume.reshape(extent_x // 2, 2, extent_y // 2, 2, extent_z // 2, 2, channels)
    grid = grid.transpose(0, 2, 4, 1, 3, 5, 6)
    return grid.reshape(extent_x * extent_y * extent_z // 8, 8 * channels)


def from_tokens(matrix, extent_x, extent_y, extent_z):
    channels = matrix.shape[1] // 8
    grid = matrix.reshape(extent_x // 2, extent_y // 2, extent_z // 2, 2, 2, 2, channels)
    grid = grid.transpose(0, 3, 1, 4, 2, 5, 6)
    return grid.reshape(extent_x, extent_y, extent_z, channels)


def plane_columns(padded, extent_x, extent_y, flipped):
    channels = padded.shape[3]
    rows = extent_x * extent_y * padded.shape[2]
    pieces = []
    for offset_x in range(3):
        for offset_y in range(3):
            start_x = 2 - offset_x if flipped else offset_x
            start_y = 2 - offset_y if flipped else offset_y
            pieces.append(
                padded[start_x : start_x + extent_x, start_y : start_y + extent_y].reshape(
                    rows, channels
                )
            )
    return jnp.concatenate(pieces, axis=1)


def depth_sum(product, extent_z, channels, flipped):
    grid = product.reshape(-1, extent_z, 3, channels)
    first, last = (2, 0) if flipped else (0, 2)
    below = jnp.pad(grid[:, :-1, first], ((0, 0), (1, 0), (0, 0)))
    above = jnp.pad(grid[:, 1:, last], ((0, 0), (0, 1), (0, 0)))
    return (below + grid[:, :, 1] + above).reshape(-1, channels)


def local(features, conv_weight, down_weight, norm_gain, qkv_weight, out_weight, upstream):
    extent_x, extent_y, extent_z, channels = features.shape
    model_width = out_weight.shape[0]
    voxels = extent_x * extent_y * extent_z
    score_scale = HD ** (-0.5)
    taps = conv_weight.reshape(9, 3, channels, channels)
    padded = padded_2(features, (("gx", 0), ("gy", 1)), 1)
    columns = plane_columns(padded, extent_x, extent_y, False)
    weight_fwd = taps.transpose(0, 2, 1, 3).reshape(9 * channels, 3 * channels)
    hidden = depth_sum(
        jnp.dot(columns, weight_fwd, preferred_element_type=jnp.float32),
        extent_z,
        channels,
        False,
    )
    gate_sig = jax.nn.sigmoid(hidden)
    activation = (hidden * gate_sig).astype(jnp.bfloat16)
    tokens_in = to_tokens(activation.reshape(extent_x, extent_y, extent_z, channels))
    tok_count = tokens_in.shape[0]
    trunk_rows = jnp.dot(tokens_in, down_weight, preferred_element_type=jnp.float32)
    mean_rows = jnp.mean(trunk_rows, axis=-1, keepdims=True)
    centred = trunk_rows - mean_rows
    inverse_std = lax.rsqrt(jnp.mean(centred * centred, axis=-1, keepdims=True) + 1e-05)
    normed = centred * inverse_std
    normed_b = (normed * norm_gain).astype(jnp.bfloat16)
    qkv_rows = jnp.dot(normed_b, qkv_weight, preferred_element_type=jnp.float32).astype(
        jnp.bfloat16
    )
    queries = qkv_rows[:, :model_width]
    local_keys = qkv_rows[:, model_width : 2 * model_width]
    local_values = qkv_rows[:, 2 * model_width :]
    gathered = lax.all_gather(
        qkv_rows[:, model_width:], ("gx", "gy"), axis=0, tiled=True
    )
    all_keys = gathered[:, :model_width]
    all_values = gathered[:, model_width:]
    queries_h = queries.reshape(tok_count, H, HD)
    keys_h = all_keys.reshape(-1, H, HD)
    values_h = all_values.reshape(-1, H, HD)
    scores = (
        jnp.einsum("ihe,jhe->hij", queries_h, keys_h, preferred_element_type=jnp.float32)
        * score_scale
    )
    exp_scores = jnp.exp(scores)
    totals = jnp.sum(exp_scores, axis=-1)
    attn_probs = exp_scores / totals[:, :, None]
    probs_b = attn_probs.astype(jnp.bfloat16)
    attended = jnp.einsum("hij,jhe->ihe", probs_b, values_h, preferred_element_type=jnp.float32)
    attended = attended.reshape(tok_count, model_width).astype(jnp.bfloat16)
    cotangent = upstream.reshape(tok_count, model_width)
    cot_float = cotangent.astype(jnp.float32)
    out_part = jnp.einsum("td,te->de", attended, cotangent, preferred_element_type=jnp.float32)
    d_attended = jnp.dot(cotangent, out_weight.T, preferred_element_type=jnp.float32).astype(
        jnp.bfloat16
    )
    d_att_h = d_attended.reshape(tok_count, H, HD)
    d_probs = jnp.einsum("ihe,jhe->hij", d_att_h, values_h, preferred_element_type=jnp.float32)
    d_probs = d_probs.astype(jnp.bfloat16).astype(jnp.float32)
    row_delta = jnp.sum(attn_probs * d_probs, axis=-1)
    d_scores = attn_probs * (d_probs - row_delta[:, :, None])
    d_queries = (
        jnp.einsum(
            "hij,jhe->ihe", d_scores, keys_h, preferred_element_type=jnp.float32
        )
        * score_scale
    )
    key_term = (
        jnp.einsum(
            "hij,ihe->jhe",
            d_scores,
            queries_h,
            preferred_element_type=jnp.float32,
        )
        * score_scale
    )
    value_term = jnp.einsum("hij,ihe->jhe", probs_b, d_att_h, preferred_element_type=jnp.float32)
    groups = lax.axis_size(("gx", "gy"))
    key_parts = jnp.concatenate(
        [
            key_term.reshape(tok_count * groups, model_width),
            value_term.reshape(tok_count * groups, model_width),
        ],
        axis=1,
    ).astype(jnp.bfloat16)
    key_parts = lax.all_to_all(key_parts, ("gx", "gy"), 0, 0, tiled=True)
    key_sums = jnp.sum(
        key_parts.reshape(groups, tok_count, 2 * model_width).astype(jnp.float32), axis=0
    )
    d_keys = key_sums[:, :model_width].astype(jnp.bfloat16)
    d_values = key_sums[:, model_width:].astype(jnp.bfloat16)
    d_qkv = jnp.concatenate(
        [d_queries.reshape(tok_count, model_width).astype(jnp.bfloat16), d_keys, d_values], axis=1
    )
    qkv_part = jnp.einsum("td,te->de", normed_b, d_qkv, preferred_element_type=jnp.float32)
    d_normed = (
        jnp.dot(d_qkv, qkv_weight.T, preferred_element_type=jnp.float32)
        .astype(jnp.bfloat16)
        .astype(jnp.float32)
    )
    d_hat = d_normed * norm_gain
    gain_part = jnp.sum(d_normed * normed, axis=0)
    d_trunk = cot_float + inverse_std * (
        d_hat
        - jnp.mean(d_hat, axis=-1, keepdims=True)
        - normed * jnp.mean(d_hat * normed, axis=-1, keepdims=True)
    )
    down_part = jnp.einsum(
        "tr,td->rd", tokens_in, d_trunk, preferred_element_type=jnp.float32
    )
    d_activation = jnp.dot(
        d_trunk, down_weight.T, preferred_element_type=jnp.float32
    ).astype(jnp.bfloat16)
    d_act_grid = (
        from_tokens(d_activation, extent_x, extent_y, extent_z)
        .reshape(voxels, channels)
        .astype(jnp.float32)
    )
    d_hidden = (d_act_grid * gate_sig * (1.0 + hidden * (1.0 - gate_sig))).astype(jnp.bfloat16)
    d_depth = d_hidden.reshape(-1, extent_z, channels)
    d_shifts = [
        jnp.pad(d_depth[:, 1:], ((0, 0), (0, 1), (0, 0))),
        d_depth,
        jnp.pad(d_depth[:, :-1], ((0, 0), (1, 0), (0, 0))),
    ]
    conv_blocks = [
        jnp.einsum(
            "vr,vc->rc",
            columns,
            shifted.reshape(voxels, channels),
            preferred_element_type=jnp.float32,
        )
        .astype(jnp.bfloat16)
        .reshape(9, channels, channels)
        for shifted in d_shifts
    ]
    conv_part = jnp.stack(conv_blocks, axis=1).reshape(27 * channels, channels)
    d_padded = padded_2(
        d_hidden.reshape(extent_x, extent_y, extent_z, channels), (("gx", 0), ("gy", 1)), 1
    )
    d_columns = plane_columns(d_padded, extent_x, extent_y, True)
    weight_bwd = taps.transpose(0, 3, 1, 2).reshape(9 * channels, 3 * channels)
    grad_features = depth_sum(
        jnp.dot(d_columns, weight_bwd, preferred_element_type=jnp.float32),
        extent_z,
        channels,
        True,
    )
    grad_features = grad_features.reshape(extent_x, extent_y, extent_z, channels).astype(
        jnp.bfloat16
    )
    groups = lax.axis_size(("gx", "gy"))
    gain_rows = gain_part.reshape(groups, -1)
    gain_high = gain_rows.astype(jnp.bfloat16)
    gain_low = (gain_rows - gain_high.astype(jnp.float32)).astype(jnp.bfloat16)
    gain_pair = jnp.concatenate([gain_high, gain_low], axis=1)
    gain_pair = jnp.pad(gain_pair, ((0, 0), (0, 1024 - gain_pair.shape[1])))
    pieces = [
        down_part.astype(jnp.bfloat16),
        qkv_part.astype(jnp.bfloat16),
        out_part.astype(jnp.bfloat16),
    ]
    shapes = [piece.shape for piece in pieces]
    flat = [piece.reshape(groups, -1, 128) for piece in pieces] + [gain_pair.reshape(groups, -1, 128)]
    heights = [piece.shape[1] for piece in flat]
    joined = jnp.concatenate(flat, axis=1)
    summed = lax.psum_scatter(
        joined.reshape(-1, 128), ("gx", "gy"), scatter_dimension=0, tiled=True
    )
    summed = lax.optimization_barrier(summed)
    results = []
    offset = 0
    for height in heights:
        results.append(summed[offset : offset + height])
        offset += height
    down_sum, qkv_sum, out_sum = [
        piece.reshape(shape[0] // groups, shape[1]) for piece, shape in zip(results[:3], shapes)
    ]
    conv_rows = lax.all_to_all(conv_part, ("gx", "gy"), 0, 0, tiled=True)
    conv_sum = jnp.sum(
        conv_rows.reshape(groups, -1, channels).astype(jnp.float32), axis=0
    )
    gain_flat = results[3].reshape(-1).astype(jnp.float32)
    half = gain_high.shape[1]
    gain_sum = gain_flat[:half] + gain_flat[half : 2 * half]
    return (
        grad_features,
        conv_sum.astype(jnp.bfloat16),
        down_sum.astype(jnp.bfloat16),
        gain_sum,
        qkv_sum.astype(jnp.bfloat16),
        out_sum.astype(jnp.bfloat16),
    )


def solution(mesh):
    placed = (
        P(("batch", "gx"), "gy", None, None),
        P(),
        P(),
        P(),
        P(),
        P(),
        P(("batch", "gx"), "gy", None, None),
    )
    return jax.shard_map(
        local,
        mesh=mesh,
        in_specs=placed,
        out_specs=(
            P(("batch", "gx"), "gy", None, None),
            P(("batch", "gx", "gy"), None),
            P(("batch", "gx", "gy"), None),
            P(("batch", "gx", "gy")),
            P(("batch", "gx", "gy"), None),
            P(("batch", "gx", "gy"), None),
        ),
        check_vma=False,
    )
```

```python
import jax
import jax.numpy as jnp
from jax import lax
from jax.sharding import PartitionSpec as P

H = 8
HD = 64


precise = lax.Precision.HIGHEST


def padded_2(block, sides, width):
    for axis, dim in sides:
        count = lax.axis_size(axis)
        forward = [(i, i + 1) for i in range(count - 1)]
        backward = [(target, source) for source, target in forward]
        low = lax.ppermute(
            lax.slice_in_dim(block, block.shape[dim] - width, None, axis=dim), axis, forward
        )
        high = lax.ppermute(lax.slice_in_dim(block, 0, width, axis=dim), axis, backward)
        block = jnp.concatenate([low, block, high], axis=dim)
    return block


def to_tokens(volume):
    extent_x, extent_y, extent_z, channels = volume.shape
    grid = volume.reshape(extent_x // 2, 2, extent_y // 2, 2, extent_z // 2, 2, channels)
    grid = grid.transpose(0, 2, 4, 1, 3, 5, 6)
    return grid.reshape(extent_x * extent_y * extent_z // 8, 8 * channels)


def from_tokens(matrix, extent_x, extent_y, extent_z):
    channels = matrix.shape[1] // 8
    grid = matrix.reshape(extent_x // 2, extent_y // 2, extent_z // 2, 2, 2, 2, channels)
    grid = grid.transpose(0, 3, 1, 4, 2, 5, 6)
    return grid.reshape(extent_x, extent_y, extent_z, channels)


def plane_columns(padded, extent_x, extent_y, flipped):
    channels = padded.shape[3]
    rows = extent_x * extent_y * padded.shape[2]
    pieces = []
    for offset_x in range(3):
        for offset_y in range(3):
            start_x = 2 - offset_x if flipped else offset_x
            start_y = 2 - offset_y if flipped else offset_y
            pieces.append(
                padded[start_x : start_x + extent_x, start_y : start_y + extent_y].reshape(
                    rows, channels
                )
            )
    return jnp.concatenate(pieces, axis=1)


def depth_sum(product, extent_z, channels, flipped):
    grid = product.reshape(-1, extent_z, 3, channels)
    first, last = (2, 0) if flipped else (0, 2)
    below = jnp.pad(grid[:, :-1, first], ((0, 0), (1, 0), (0, 0)))
    above = jnp.pad(grid[:, 1:, last], ((0, 0), (0, 1), (0, 0)))
    return (below + grid[:, :, 1] + above).reshape(-1, channels)


def local(features, conv_weight, down_weight, norm_gain, qkv_weight, out_weight, upstream):
    extent_x, extent_y, extent_z, channels = features.shape
    model_width = out_weight.shape[0]
    voxels = extent_x * extent_y * extent_z
    score_scale = HD ** (-0.5)
    taps = conv_weight.reshape(9, 3, channels, channels)
    padded = padded_2(features, (("gx", 0), ("gy", 1)), 1)
    columns = plane_columns(padded, extent_x, extent_y, False)
    weight_fwd = taps.transpose(0, 2, 1, 3).reshape(9 * channels, 3 * channels)
    hidden = depth_sum(
        jnp.dot(columns, weight_fwd, preferred_element_type=jnp.float32),
        extent_z,
        channels,
        False,
    )
    gate_sig = jax.nn.sigmoid(hidden)
    activation = (hidden * gate_sig).astype(jnp.bfloat16)
    tokens_in = to_tokens(activation.reshape(extent_x, extent_y, extent_z, channels))
    tok_count = tokens_in.shape[0]
    trunk_rows = jnp.dot(tokens_in, down_weight, preferred_element_type=jnp.float32)
    mean_rows = jnp.mean(trunk_rows, axis=-1, keepdims=True)
    centred = trunk_rows - mean_rows
    inverse_std = lax.rsqrt(jnp.mean(centred * centred, axis=-1, keepdims=True) + 1e-05)
    normed = centred * inverse_std
    normed_b = (normed * norm_gain).astype(jnp.bfloat16)
    qkv_rows = jnp.dot(normed_b, qkv_weight, preferred_element_type=jnp.float32).astype(
        jnp.bfloat16
    )
    queries = qkv_rows[:, :model_width]
    local_keys = qkv_rows[:, model_width : 2 * model_width]
    local_values = qkv_rows[:, 2 * model_width :]
    gathered = lax.all_gather(
        qkv_rows[:, model_width:], ("gx", "gy"), axis=0, tiled=True
    )
    all_keys = gathered[:, :model_width]
    all_values = gathered[:, model_width:]
    queries_h = queries.reshape(tok_count, H, HD)
    keys_h = all_keys.reshape(-1, H, HD)
    values_h = all_values.reshape(-1, H, HD)
    scores = (
        jnp.einsum("ihe,jhe->hij", queries_h, keys_h, preferred_element_type=jnp.float32)
        * score_scale
    )
    exp_scores = jnp.exp(scores)
    totals = jnp.sum(exp_scores, axis=-1)
    attn_probs = exp_scores / totals[:, :, None]
    probs_b = attn_probs.astype(jnp.bfloat16)
    attended = jnp.einsum("hij,jhe->ihe", probs_b, values_h, preferred_element_type=jnp.float32)
    attended = attended.reshape(tok_count, model_width).astype(jnp.bfloat16)
    cotangent = upstream.reshape(tok_count, model_width)
    cot_float = cotangent.astype(jnp.float32)
    out_part = jnp.einsum("td,te->de", attended, cotangent, preferred_element_type=jnp.float32)
    d_attended = jnp.dot(cotangent, out_weight.T, preferred_element_type=jnp.float32).astype(
        jnp.bfloat16
    )
    d_att_h = d_attended.reshape(tok_count, H, HD)
    d_probs = jnp.einsum("ihe,jhe->hij", d_att_h, values_h, preferred_element_type=jnp.float32)
    d_probs = d_probs.astype(jnp.bfloat16).astype(jnp.float32)
    row_delta = jnp.sum(attn_probs * d_probs, axis=-1)
    d_scores = (attn_probs * (d_probs - row_delta[:, :, None])).astype(jnp.bfloat16)
    d_queries = (
        jnp.einsum(
            "hij,jhe->ihe", d_scores, keys_h, preferred_element_type=jnp.float32
        )
        * score_scale
    )
    key_term = (
        jnp.einsum(
            "hij,ihe->jhe",
            d_scores,
            queries_h,
            preferred_element_type=jnp.float32,
        )
        * score_scale
    )
    value_term = jnp.einsum("hij,ihe->jhe", probs_b, d_att_h, preferred_element_type=jnp.float32)
    groups = lax.axis_size(("gx", "gy"))
    key_parts = jnp.concatenate(
        [
            key_term.reshape(tok_count * groups, model_width),
            value_term.reshape(tok_count * groups, model_width),
        ],
        axis=1,
    ).astype(jnp.bfloat16)
    key_parts = lax.all_to_all(key_parts, ("gx", "gy"), 0, 0, tiled=True)
    key_sums = jnp.sum(
        key_parts.reshape(groups, tok_count, 2 * model_width).astype(jnp.float32), axis=0
    )
    d_keys = key_sums[:, :model_width].astype(jnp.bfloat16)
    d_values = key_sums[:, model_width:].astype(jnp.bfloat16)
    d_qkv = jnp.concatenate(
        [d_queries.reshape(tok_count, model_width).astype(jnp.bfloat16), d_keys, d_values], axis=1
    )
    qkv_part = jnp.einsum("td,te->de", normed_b, d_qkv, preferred_element_type=jnp.float32)
    d_normed = (
        jnp.dot(d_qkv, qkv_weight.T, preferred_element_type=jnp.float32)
        .astype(jnp.bfloat16)
        .astype(jnp.float32)
    )
    d_hat = d_normed * norm_gain
    gain_part = jnp.sum(d_normed * normed, axis=0)
    d_trunk = cot_float + inverse_std * (
        d_hat
        - jnp.mean(d_hat, axis=-1, keepdims=True)
        - normed * jnp.mean(d_hat * normed, axis=-1, keepdims=True)
    )
    down_part = jnp.einsum(
        "tr,td->rd", tokens_in, d_trunk, preferred_element_type=jnp.float32
    )
    d_activation = jnp.dot(
        d_trunk, down_weight.T, preferred_element_type=jnp.float32
    ).astype(jnp.bfloat16)
    d_act_grid = (
        from_tokens(d_activation, extent_x, extent_y, extent_z)
        .reshape(voxels, channels)
        .astype(jnp.float32)
    )
    d_hidden = (d_act_grid * gate_sig * (1.0 + hidden * (1.0 - gate_sig))).astype(jnp.bfloat16)
    d_depth = d_hidden.reshape(-1, extent_z, channels)
    d_shifts = [
        jnp.pad(d_depth[:, 1:], ((0, 0), (0, 1), (0, 0))),
        d_depth,
        jnp.pad(d_depth[:, :-1], ((0, 0), (1, 0), (0, 0))),
    ]
    conv_blocks = [
        jnp.einsum(
            "vr,vc->rc",
            columns,
            shifted.reshape(voxels, channels),
            preferred_element_type=jnp.float32,
        )
        .astype(jnp.bfloat16)
        .reshape(9, channels, channels)
        for shifted in d_shifts
    ]
    conv_part = jnp.stack(conv_blocks, axis=1).reshape(27 * channels, channels)
    d_padded = padded_2(
        d_hidden.reshape(extent_x, extent_y, extent_z, channels), (("gx", 0), ("gy", 1)), 1
    )
    d_columns = plane_columns(d_padded, extent_x, extent_y, True)
    weight_bwd = taps.transpose(0, 3, 1, 2).reshape(9 * channels, 3 * channels)
    grad_features = depth_sum(
        jnp.dot(d_columns, weight_bwd, preferred_element_type=jnp.float32),
        extent_z,
        channels,
        True,
    )
    grad_features = grad_features.reshape(extent_x, extent_y, extent_z, channels).astype(
        jnp.bfloat16
    )
    groups = lax.axis_size(("gx", "gy"))
    gain_rows = gain_part.reshape(groups, -1)
    gain_high = gain_rows.astype(jnp.bfloat16)
    gain_low = (gain_rows - gain_high.astype(jnp.float32)).astype(jnp.bfloat16)
    gain_pair = jnp.concatenate([gain_high, gain_low], axis=1)
    gain_pair = jnp.pad(gain_pair, ((0, 0), (0, 1024 - gain_pair.shape[1])))
    pieces = [
        down_part.astype(jnp.bfloat16),
        qkv_part.astype(jnp.bfloat16),
        out_part.astype(jnp.bfloat16),
    ]
    shapes = [piece.shape for piece in pieces]
    flat = [piece.reshape(groups, -1, 128) for piece in pieces] + [gain_pair.reshape(groups, -1, 128)]
    heights = [piece.shape[1] for piece in flat]
    joined = jnp.concatenate(flat, axis=1)
    summed = lax.psum_scatter(
        joined.reshape(-1, 128), ("gx", "gy"), scatter_dimension=0, tiled=True
    )
    summed = lax.optimization_barrier(summed)
    results = []
    offset = 0
    for height in heights:
        results.append(summed[offset : offset + height])
        offset += height
    down_sum, qkv_sum, out_sum = [
        piece.reshape(shape[0] // groups, shape[1]) for piece, shape in zip(results[:3], shapes)
    ]
    conv_rows = lax.all_to_all(conv_part, ("gx", "gy"), 0, 0, tiled=True)
    conv_sum = jnp.sum(
        conv_rows.reshape(groups, -1, channels).astype(jnp.float32), axis=0
    )
    gain_flat = results[3].reshape(-1).astype(jnp.float32)
    half = gain_high.shape[1]
    gain_sum = gain_flat[:half] + gain_flat[half : 2 * half]
    return (
        grad_features,
        conv_sum.astype(jnp.bfloat16),
        down_sum.astype(jnp.bfloat16),
        gain_sum,
        qkv_sum.astype(jnp.bfloat16),
        out_sum.astype(jnp.bfloat16),
    )


def solution(mesh):
    placed = (
        P(("batch", "gx"), "gy", None, None),
        P(),
        P(),
        P(),
        P(),
        P(),
        P(("batch", "gx"), "gy", None, None),
    )
    return jax.shard_map(
        local,
        mesh=mesh,
        in_specs=placed,
        out_specs=(
            P(("batch", "gx"), "gy", None, None),
            P(("batch", "gx", "gy"), None),
            P(("batch", "gx", "gy"), None),
            P(("batch", "gx", "gy")),
            P(("batch", "gx", "gy"), None),
            P(("batch", "gx", "gy"), None),
        ),
        check_vma=False,
    )
```

```python
import jax
import jax.numpy as jnp
from jax import lax
from jax.sharding import PartitionSpec as P

H = 8
HD = 64


precise = lax.Precision.HIGHEST


def padded_2(block, sides, width):
    for axis, dim in sides:
        count = lax.axis_size(axis)
        forward = [(i, i + 1) for i in range(count - 1)]
        backward = [(target, source) for source, target in forward]
        low = lax.ppermute(
            lax.slice_in_dim(block, block.shape[dim] - width, None, axis=dim), axis, forward
        )
        high = lax.ppermute(lax.slice_in_dim(block, 0, width, axis=dim), axis, backward)
        block = jnp.concatenate([low, block, high], axis=dim)
    return block


def to_tokens(volume):
    extent_x, extent_y, extent_z, channels = volume.shape
    grid = volume.reshape(extent_x // 2, 2, extent_y // 2, 2, extent_z // 2, 2, channels)
    grid = grid.transpose(0, 2, 4, 1, 3, 5, 6)
    return grid.reshape(extent_x * extent_y * extent_z // 8, 8 * channels)


def from_tokens(matrix, extent_x, extent_y, extent_z):
    channels = matrix.shape[1] // 8
    grid = matrix.reshape(extent_x // 2, extent_y // 2, extent_z // 2, 2, 2, 2, channels)
    grid = grid.transpose(0, 3, 1, 4, 2, 5, 6)
    return grid.reshape(extent_x, extent_y, extent_z, channels)


def plane_columns(padded, extent_x, extent_y, flipped):
    channels = padded.shape[3]
    rows = extent_x * extent_y * padded.shape[2]
    pieces = []
    for offset_x in range(3):
        for offset_y in range(3):
            start_x = 2 - offset_x if flipped else offset_x
            start_y = 2 - offset_y if flipped else offset_y
            pieces.append(
                padded[start_x : start_x + extent_x, start_y : start_y + extent_y].reshape(
                    rows, channels
                )
            )
    return jnp.concatenate(pieces, axis=1)


def depth_sum(product, extent_z, channels, flipped):
    grid = product.reshape(-1, extent_z, 3, channels)
    first, last = (2, 0) if flipped else (0, 2)
    below = jnp.pad(grid[:, :-1, first], ((0, 0), (1, 0), (0, 0)))
    above = jnp.pad(grid[:, 1:, last], ((0, 0), (0, 1), (0, 0)))
    return (below + grid[:, :, 1] + above).reshape(-1, channels)


def local(features, conv_weight, down_weight, norm_gain, qkv_weight, out_weight, upstream):
    extent_x, extent_y, extent_z, channels = features.shape
    model_width = out_weight.shape[0]
    voxels = extent_x * extent_y * extent_z
    score_scale = HD ** (-0.5)
    taps = conv_weight.reshape(9, 3, channels, channels)
    padded = padded_2(features, (("gx", 0), ("gy", 1)), 1)
    columns = plane_columns(padded, extent_x, extent_y, False)
    weight_fwd = taps.transpose(0, 2, 1, 3).reshape(9 * channels, 3 * channels)
    hidden = depth_sum(
        jnp.dot(columns, weight_fwd, preferred_element_type=jnp.float32),
        extent_z,
        channels,
        False,
    )
    gate_sig = jax.nn.sigmoid(hidden)
    activation = (hidden * gate_sig).astype(jnp.bfloat16)
    tokens_in = to_tokens(activation.reshape(extent_x, extent_y, extent_z, channels))
    tok_count = tokens_in.shape[0]
    trunk_rows = jnp.dot(tokens_in, down_weight, preferred_element_type=jnp.float32)
    mean_rows = jnp.mean(trunk_rows, axis=-1, keepdims=True)
    centred = trunk_rows - mean_rows
    inverse_std = lax.rsqrt(jnp.mean(centred * centred, axis=-1, keepdims=True) + 1e-05)
    normed = centred * inverse_std
    normed_b = (normed * norm_gain).astype(jnp.bfloat16)
    qkv_rows = jnp.dot(normed_b, qkv_weight, preferred_element_type=jnp.float32).astype(
        jnp.bfloat16
    )
    queries = qkv_rows[:, :model_width]
    local_keys = qkv_rows[:, model_width : 2 * model_width]
    local_values = qkv_rows[:, 2 * model_width :]
    gathered = lax.all_gather(
        qkv_rows[:, model_width:], ("gx", "gy"), axis=0, tiled=True
    )
    all_keys = gathered[:, :model_width]
    all_values = gathered[:, model_width:]
    queries_h = queries.reshape(tok_count, H, HD)
    keys_h = all_keys.reshape(-1, H, HD)
    values_h = all_values.reshape(-1, H, HD)
    scores = (
        jnp.einsum("ihe,jhe->hij", queries_h, keys_h, preferred_element_type=jnp.float32)
        * score_scale
    )
    exp_scores = jnp.exp(scores)
    totals = jnp.sum(exp_scores, axis=-1)
    attn_probs = exp_scores * (1.0 / totals)[:, :, None]
    probs_b = attn_probs.astype(jnp.bfloat16)
    attended = jnp.einsum("hij,jhe->ihe", probs_b, values_h, preferred_element_type=jnp.float32)
    attended = attended.reshape(tok_count, model_width).astype(jnp.bfloat16)
    cotangent = upstream.reshape(tok_count, model_width)
    cot_float = cotangent.astype(jnp.float32)
    out_part = jnp.einsum("td,te->de", attended, cotangent, preferred_element_type=jnp.float32)
    d_attended = jnp.dot(cotangent, out_weight.T, preferred_element_type=jnp.float32).astype(
        jnp.bfloat16
    )
    d_att_h = d_attended.reshape(tok_count, H, HD)
    d_probs = jnp.einsum("ihe,jhe->hij", d_att_h, values_h, preferred_element_type=jnp.float32)
    d_probs = d_probs.astype(jnp.bfloat16).astype(jnp.float32)
    row_delta = jnp.sum(attn_probs * d_probs, axis=-1)
    d_scores = attn_probs * (d_probs - row_delta[:, :, None])
    d_queries = (
        jnp.einsum(
            "hij,jhe->ihe", d_scores, keys_h, preferred_element_type=jnp.float32
        )
        * score_scale
    )
    key_term = (
        jnp.einsum(
            "hij,ihe->jhe",
            d_scores,
            queries_h,
            preferred_element_type=jnp.float32,
        )
        * score_scale
    )
    value_term = jnp.einsum("hij,ihe->jhe", probs_b, d_att_h, preferred_element_type=jnp.float32)
    groups = lax.axis_size(("gx", "gy"))
    key_parts = jnp.concatenate(
        [
            key_term.reshape(tok_count * groups, model_width),
            value_term.reshape(tok_count * groups, model_width),
        ],
        axis=1,
    ).astype(jnp.bfloat16)
    key_parts = lax.all_to_all(key_parts, ("gx", "gy"), 0, 0, tiled=True)
    key_sums = jnp.sum(
        key_parts.reshape(groups, tok_count, 2 * model_width).astype(jnp.float32), axis=0
    )
    d_keys = key_sums[:, :model_width].astype(jnp.bfloat16)
    d_values = key_sums[:, model_width:].astype(jnp.bfloat16)
    d_qkv = jnp.concatenate(
        [d_queries.reshape(tok_count, model_width).astype(jnp.bfloat16), d_keys, d_values], axis=1
    )
    qkv_part = jnp.einsum("td,te->de", normed_b, d_qkv, preferred_element_type=jnp.float32)
    d_normed = (
        jnp.dot(d_qkv, qkv_weight.T, preferred_element_type=jnp.float32)
        .astype(jnp.bfloat16)
        .astype(jnp.float32)
    )
    d_hat = d_normed * norm_gain
    gain_part = jnp.sum(d_normed * normed, axis=0)
    d_trunk = cot_float + inverse_std * (
        d_hat
        - jnp.mean(d_hat, axis=-1, keepdims=True)
        - normed * jnp.mean(d_hat * normed, axis=-1, keepdims=True)
    )
    down_part = jnp.einsum(
        "tr,td->rd", tokens_in, d_trunk, preferred_element_type=jnp.float32
    )
    d_activation = jnp.dot(
        d_trunk, down_weight.T, preferred_element_type=jnp.float32
    ).astype(jnp.bfloat16)
    d_act_grid = (
        from_tokens(d_activation, extent_x, extent_y, extent_z)
        .reshape(voxels, channels)
        .astype(jnp.float32)
    )
    d_hidden = (d_act_grid * gate_sig * (1.0 + hidden * (1.0 - gate_sig))).astype(jnp.bfloat16)
    d_depth = d_hidden.reshape(-1, extent_z, channels)
    d_shifts = [
        jnp.pad(d_depth[:, 1:], ((0, 0), (0, 1), (0, 0))),
        d_depth,
        jnp.pad(d_depth[:, :-1], ((0, 0), (1, 0), (0, 0))),
    ]
    conv_blocks = [
        jnp.einsum(
            "vr,vc->rc",
            columns,
            shifted.reshape(voxels, channels),
            preferred_element_type=jnp.float32,
        )
        .astype(jnp.bfloat16)
        .reshape(9, channels, channels)
        for shifted in d_shifts
    ]
    conv_part = jnp.stack(conv_blocks, axis=1).reshape(27 * channels, channels)
    d_padded = padded_2(
        d_hidden.reshape(extent_x, extent_y, extent_z, channels), (("gx", 0), ("gy", 1)), 1
    )
    d_columns = plane_columns(d_padded, extent_x, extent_y, True)
    weight_bwd = taps.transpose(0, 3, 1, 2).reshape(9 * channels, 3 * channels)
    grad_features = depth_sum(
        jnp.dot(d_columns, weight_bwd, preferred_element_type=jnp.float32),
        extent_z,
        channels,
        True,
    )
    grad_features = grad_features.reshape(extent_x, extent_y, extent_z, channels).astype(
        jnp.bfloat16
    )
    groups = lax.axis_size(("gx", "gy"))
    gain_rows = gain_part.reshape(groups, -1)
    gain_high = gain_rows.astype(jnp.bfloat16)
    gain_low = (gain_rows - gain_high.astype(jnp.float32)).astype(jnp.bfloat16)
    gain_pair = jnp.concatenate([gain_high, gain_low], axis=1)
    gain_pair = jnp.pad(gain_pair, ((0, 0), (0, 1024 - gain_pair.shape[1])))
    pieces = [
        down_part.astype(jnp.bfloat16),
        qkv_part.astype(jnp.bfloat16),
        out_part.astype(jnp.bfloat16),
    ]
    shapes = [piece.shape for piece in pieces]
    flat = [piece.reshape(groups, -1, 128) for piece in pieces] + [gain_pair.reshape(groups, -1, 128)]
    heights = [piece.shape[1] for piece in flat]
    joined = jnp.concatenate(flat, axis=1)
    summed = lax.psum_scatter(
        joined.reshape(-1, 128), ("gx", "gy"), scatter_dimension=0, tiled=True
    )
    summed = lax.optimization_barrier(summed)
    results = []
    offset = 0
    for height in heights:
        results.append(summed[offset : offset + height])
        offset += height
    down_sum, qkv_sum, out_sum = [
        piece.reshape(shape[0] // groups, shape[1]) for piece, shape in zip(results[:3], shapes)
    ]
    conv_rows = lax.all_to_all(conv_part, ("gx", "gy"), 0, 0, tiled=True)
    conv_sum = jnp.sum(
        conv_rows.reshape(groups, -1, channels).astype(jnp.float32), axis=0
    )
    gain_flat = results[3].reshape(-1).astype(jnp.float32)
    half = gain_high.shape[1]
    gain_sum = gain_flat[:half] + gain_flat[half : 2 * half]
    return (
        grad_features,
        conv_sum.astype(jnp.bfloat16),
        down_sum.astype(jnp.bfloat16),
        gain_sum,
        qkv_sum.astype(jnp.bfloat16),
        out_sum.astype(jnp.bfloat16),
    )


def solution(mesh):
    placed = (
        P(("batch", "gx"), "gy", None, None),
        P(),
        P(),
        P(),
        P(),
        P(),
        P(("batch", "gx"), "gy", None, None),
    )
    return jax.shard_map(
        local,
        mesh=mesh,
        in_specs=placed,
        out_specs=(
            P(("batch", "gx"), "gy", None, None),
            P(("batch", "gx", "gy"), None),
            P(("batch", "gx", "gy"), None),
            P(("batch", "gx", "gy")),
            P(("batch", "gx", "gy"), None),
            P(("batch", "gx", "gy"), None),
        ),
        check_vma=False,
    )
```
